32 devices in a mesh: grp: 2 (over y), tm: 4 (over z), height: 4 (over x, core).
Axes of the slice: x: 2, y: 2, z: 4, core: 2. Of those that a mesh axis runs over, the one named last changes fastest.
Arguments:
- latents: bfloat16 [8, 8, 160, 384], P(('grp', 'tm'), 'height'), parts along dimension 0, may hold values from -6 to 6
- gain: float32 [384], replicated, may hold values from 0.1 to 1.9
- bias: float32 [384], replicated, may hold values from -3 to 3
- weight: bfloat16 [10368, 384], replicated, may hold values from -0.0625 to 0.0625
- cotangent: bfloat16 [8, 8, 160, 384], P(('grp', 'tm'), 'height'), parts along dimension 0, may hold values from -6 to 6
Outputs:
- output: bfloat16 [8, 8, 160, 384], P(('grp', 'tm'), 'height'), parts along dimension 0
- latent_grad: bfloat16 [8, 8, 160, 384], P(('grp', 'tm'), 'height'), parts along dimension 0
- weight_grad: float32 [20736, 384], P(('grp', 'tm'), 'height'), parts along dimension 0
The draws below stay inside these ranges and needn't reach their ends.
There are 2 independent parts, one for each index of `grp`. The reference program is written for one: setup_inputs(seed, part) draws one part's arguments, and reference() takes and returns one part's arrays. A program takes and returns all parts, laid end to end along the dimension named above; an argument that names none is the same for every part. Nothing has to cross between parts.
All inputs are finite; a program needn't handle non-finite values.
Results may differ from the reference program's by a relative error of at most 0.0029.
Values may be sent and summed in bfloat16 or wider, within the bound.
No kernel may reach another device: no remote copies, remote signals or barrier semaphores. Data moves between devices by JAX's collectives and lax.ppermute only.
A program may use at most 128 MiB of HBM per device.

```python
import math
import jax
import jax.numpy as jnp
from jax import lax

C = 384
W = 160
H = 8
F = 4


def steps_of(key, dims, cuts, least, high):
    level, own = 1.0, jax.random.fold_in(key, 6)
    for position, blocks in cuts:
        heights = jnp.exp(jax.random.uniform(jax.random.fold_in(own, position), (blocks,), jnp.float32, least / len(cuts), high / len(cuts)))
        level = level * jnp.repeat(heights, dims[position] // blocks).reshape([-1 if axis == position else 1 for axis in range(len(dims))])
    return level


def centred(rng, dims, width, bound, split=(), kind=jnp.bfloat16):
    array = jax.random.normal(rng, dims, jnp.float32) * width
    if len(split) > 0:
        array = steps_of(rng, dims, split, -0.22, 0.18) * array
    return jnp.clip(array, min=-bound, max=bound).astype(kind)


def setup_inputs(seed: int = 0, part: int = 0) -> dict:
    arg_keys = jax.random.split(jax.random.key(seed), 6)
    part_splits = jax.random.split(jax.random.fold_in(arg_keys[5], part), 6)
    return {
        "latents": centred(part_splits[0], (F, H, W, C), 1.0, 6.0, ((0, 4), (1, 4))),
        "gain": jnp.clip(1.0 + 0.18 * jax.random.normal(arg_keys[1], (C,), jnp.float32), 0.1, 1.9),
        "bias": centred(arg_keys[2], (C,), 0.5, 3.0, (), jnp.float32),
        "weight": centred(arg_keys[3], (27 * C, C), (27 * C) ** -0.5, 0.0625),
        "cotangent": centred(part_splits[4], (F, H, W, C), 1.0, 6.0, ((0, 4), (1, 4))),
    }


def gather_taps(frame_block, row_count, col_count, reverse_taps):
    pieces = []
    for depth_tap in range(3):
        for row_tap in range(3):
            for col_tap in range(3):
                if reverse_taps:
                    piece = frame_block[2 - depth_tap, 2 - row_tap:2 - row_tap + row_count, 2 - col_tap:2 - col_tap + col_count, :]
                else:
                    piece = frame_block[depth_tap, row_tap:row_tap + row_count, col_tap:col_tap + col_count, :]
                pieces.append(piece)
    joined = jnp.concatenate(pieces, axis=-1)
    return joined.reshape(row_count * col_count, joined.shape[-1])

def reference(latents, gain, bias, weight, cotangent):
    frame_count, row_count, col_count, channels = latents.shape
    latent_wide = latents.astype(jnp.float32)
    root_mean = jnp.sqrt(lax.optimization_barrier(jnp.mean(latent_wide * latent_wide, axis=-1, keepdims=True)) + 1e-06)
    normed = latent_wide / root_mean * gain
    hidden = jax.nn.silu(normed).astype(jnp.bfloat16)
    hidden_padded = jnp.pad(hidden, ((2, 0), (1, 1), (1, 1), (0, 0)))
    future_padded = jnp.pad(cotangent, ((0, 2), (1, 1), (1, 1), (0, 0)))
    weight_flipped = weight.reshape(27, channels, channels).transpose(0, 2, 1).reshape(27 * channels, channels)

    def frame_step(running, frame_index):
        window = lax.dynamic_slice_in_dim(hidden_padded, frame_index, 3, 0)
        future_block = lax.dynamic_slice_in_dim(future_padded, frame_index, 3, 0)
        hidden_patch = gather_taps(window, row_count, col_count, False)
        cotangent_patch = gather_taps(future_block, row_count, col_count, True)
        conv_out = jnp.dot(hidden_patch, weight, preferred_element_type=jnp.float32)
        hidden_grad = jnp.dot(cotangent_patch, weight_flipped, preferred_element_type=jnp.float32)
        cotangent_flat = lax.dynamic_index_in_dim(cotangent, frame_index, 0, keepdims=False).reshape(row_count * col_count, channels)
        running = running + lax.dot_general(hidden_patch, cotangent_flat, (((0,), (0,)), ((), ())), preferred_element_type=jnp.float32)
        return (running, (conv_out.reshape(row_count, col_count, channels), hidden_grad.reshape(row_count, col_count, channels)))
    running, (conv_out, hidden_grad) = lax.scan(frame_step, jnp.zeros((27 * channels, channels), jnp.float32), jnp.arange(frame_count, dtype=jnp.int32))
    output = (latent_wide + conv_out + bias).astype(jnp.bfloat16)
    sigmoid_pre = jax.nn.sigmoid(normed)
    normed_grad = hidden_grad * sigmoid_pre * (1.0 + normed * (1.0 - sigmoid_pre))
    scaled_grad = normed_grad * gain
    unit_latent = latent_wide / root_mean
    inner = lax.optimization_barrier(jnp.mean(scaled_grad * unit_latent, axis=-1, keepdims=True))
    latent_grad = (cotangent.astype(jnp.float32) + (scaled_grad - unit_latent * inner) / root_mean).astype(jnp.bfloat16)
    inverse_root = 1.0 / math.sqrt(frame_count * row_count * col_count)
    weight_grad = running * inverse_root
    return (output, latent_grad, weight_grad)
```

```python
import math

import jax
import jax.numpy as jnp
from jax import lax
from jax.sharding import PartitionSpec as P


def shifted_2(value, axis, by):
    devices = lax.axis_size(axis)
    pairs = [(i, i + by) for i in range(devices) if 0 <= i + by < devices]
    return lax.ppermute(value, axis, pairs)


def padded(cells, sides, width):
    for axis, dim in sides:
        count = lax.axis_size(axis)
        ends = count - 1
        head = lax.slice_in_dim(cells, 0, width, axis=dim)
        tail = lax.slice_in_dim(cells, cells.shape[dim] - width, cells.shape[dim], axis=dim)
        cells = jnp.concatenate(
            [
                lax.ppermute(tail, axis, [(i, (i + 1) % count) for i in range(ends)]),
                cells,
                lax.ppermute(head, axis, [((i + 1) % count, i) for i in range(ends)]),
            ],
            axis=dim,
        )
    return cells


def forward_arrange(cube):
    depth, rows_t, cols_t, inputs, outputs = cube.shape
    return cube.transpose(0, 1, 3, 2, 4).reshape(9, inputs, 3 * outputs)


def backward_arrange(cube):
    depth, rows_t, cols_t, inputs, outputs = cube.shape
    return cube.transpose(0, 1, 4, 2, 3).reshape(9, outputs, 3 * inputs)


def forward_sum(window, arranged, row_total, col_total):
    width = window.shape[-1]
    slots = arranged.shape[-1] // 3
    total = None
    for depth_tap in range(3):
        for row_tap in range(3):
            slab = window[depth_tap, row_tap : row_tap + row_total].reshape(
                row_total * (col_total + 2), width
            )
            product = jnp.dot(
                slab, arranged[3 * depth_tap + row_tap], preferred_element_type=jnp.float32
            )
            total = product if total is None else total + product
    total = total.reshape(row_total, col_total + 2, 3, slots)
    return (
        total[:, 0:col_total, 0] + total[:, 1 : col_total + 1, 1] + total[:, 2 : col_total + 2, 2]
    )


def backward_sum(window, arranged, row_total, col_total):
    width = window.shape[-1]
    slots = arranged.shape[-1] // 3
    total = None
    for depth_tap in range(3):
        for row_tap in range(3):
            slab = window[2 - depth_tap, 2 - row_tap : 2 - row_tap + row_total].reshape(
                row_total * (col_total + 2), width
            )
            product = jnp.dot(
                slab, arranged[3 * depth_tap + row_tap], preferred_element_type=jnp.float32
            )
            total = product if total is None else total + product
    total = total.reshape(row_total, col_total + 2, 3, slots)
    return (
        total[:, 2 : col_total + 2, 0] + total[:, 1 : col_total + 1, 1] + total[:, 0:col_total, 2]
    )


def pair_count(tap_rows, share_rows, pair_rows, parts):
    most = 1
    for index in range(parts):
        first = index * share_rows
        last = first + share_rows - 1
        most = max(most, last // pair_rows - first // pair_rows + 1)
    return most


def block_weight_grad(framed, cot_all, frame_index, share_rows, channels):
    frame_total, row_total, col_total, slots = cot_all.shape
    pair_rows = 3 * channels
    tap_rows = 27 * channels
    flat_count = frame_total * row_total * (col_total + 2)
    shifted = jnp.concatenate(
        [
            jnp.pad(cot_all, ((0, 0), (0, 0), (col_tap, 2 - col_tap), (0, 0)))
            for col_tap in range(3)
        ],
        axis=-1,
    ).reshape(flat_count, 3 * slots)
    first_row = frame_index * share_rows
    first_pair = first_row // pair_rows
    count = pair_count(tap_rows, share_rows, pair_rows, tap_rows // share_rows)
    pieces = []
    for step in range(count):
        pair = jnp.minimum(first_pair + step, 8)
        depth_tap = pair // 3
        row_tap = pair % 3
        slab = lax.dynamic_slice(
            framed,
            (depth_tap, row_tap, 0, 0),
            (frame_total, row_total, col_total + 2, channels),
        ).reshape(flat_count, channels)
        product = lax.dot_general(
            slab, shifted, (((0,), (0,)), ((), ())), preferred_element_type=jnp.float32
        )
        pieces.append(product.reshape(channels, 3, slots).transpose(1, 0, 2).reshape(pair_rows, slots))
    stacked = jnp.concatenate(pieces, axis=0)
    return lax.dynamic_slice_in_dim(stacked, first_row - first_pair * pair_rows, share_rows, 0)


def local(latents, gain, bias, weight, cotangent):
    frame_count, row_count, col_count, channels = latents.shape
    latent_wide = latents.astype(jnp.float32)
    root_mean = jnp.sqrt(jnp.mean(latent_wide * latent_wide, axis=-1, keepdims=True) + 1e-06)
    normed = latent_wide / root_mean * gain
    hidden = jax.nn.silu(normed).astype(jnp.bfloat16)
    height_count = lax.axis_size("height")
    frame_devices = lax.axis_size("tm")
    share_width = channels // height_count
    frame_index = lax.axis_index("tm")
    row_index = lax.axis_index("height")
    total_rows = row_count * height_count
    total_frames = frame_count * frame_devices
    tap_rows = 27 * channels
    share_rows = tap_rows // frame_devices
    inverse_root = 1.0 / math.sqrt(total_frames * total_rows * col_count)
    weight_cube = weight.reshape(3, 3, 3, channels, channels)

    hidden_all = lax.all_gather(hidden, ("tm", "height"), axis=0, tiled=True).reshape(
        total_frames, total_rows, col_count, channels
    )
    framed = jnp.pad(hidden_all, ((2, 0), (1, 1), (1, 1), (0, 0)))

    shared_cot = lax.all_to_all(cotangent, "height", split_axis=3, concat_axis=1, tiled=True)
    cot_all = lax.all_gather(shared_cot, "tm", axis=0, tiled=True)

    window = lax.dynamic_slice(
        framed,
        (frame_index * frame_count, row_index * row_count, 0, 0),
        (frame_count + 2, row_count + 2, col_count + 2, channels),
    )
    conv_out = forward_sum(window, forward_arrange(weight_cube), row_count, col_count).reshape(
        frame_count, row_count, col_count, channels
    )
    output = (latent_wide + conv_out + bias).astype(jnp.bfloat16)

    weight_grad = block_weight_grad(framed, cot_all, frame_index, share_rows, channels) * inverse_root

    cotangent_edged = padded(cotangent, (("height", 1),), 1)
    next_frame = shifted_2(cotangent_edged, "tm", -1)
    second_next = shifted_2(cotangent_edged, "tm", -2)
    future_block = jnp.pad(
        jnp.concatenate([cotangent_edged, next_frame, second_next], axis=0),
        ((0, 0), (0, 0), (1, 1), (0, 0)),
    )
    hidden_grad = backward_sum(
        future_block, backward_arrange(weight_cube), row_count, col_count
    ).reshape(frame_count, row_count, col_count, channels)
    sigmoid_pre = jax.nn.sigmoid(normed)
    normed_grad = hidden_grad * sigmoid_pre * (1.0 + normed * (1.0 - sigmoid_pre))
    scaled_grad = normed_grad * gain
    unit_latent = latent_wide / root_mean
    inner = jnp.mean(scaled_grad * unit_latent, axis=-1, keepdims=True)
    latent_grad = (
        cotangent.astype(jnp.float32) + (scaled_grad - unit_latent * inner) / root_mean
    ).astype(jnp.bfloat16)
    return (output, latent_grad, weight_grad)


def solution(mesh):
    placed = (
        P(("grp", "tm"), "height", None, None),
        P(),
        P(),
        P(),
        P(("grp", "tm"), "height", None, None),
    )
    return jax.shard_map(
        local,
        mesh=mesh,
        in_specs=placed,
        out_specs=(
            P(("grp", "tm"), "height", None, None),
            P(("grp", "tm"), "height", None, None),
            P(("grp", "tm"), "height"),
        ),
        check_vma=False,
    )
```

```python
import math

import jax
import jax.numpy as jnp
from jax import lax
from jax.sharding import PartitionSpec as P


def shifted_2(value, axis, by):
    devices = lax.axis_size(axis)
    pairs = [(i, i + by) for i in range(devices) if 0 <= i + by < devices]
    return lax.ppermute(value, axis, pairs)


def padded(cells, sides, width):
    for axis, dim in sides:
        count = lax.axis_size(axis)
        ends = count - 1
        head = lax.slice_in_dim(cells, 0, width, axis=dim)
        tail = lax.slice_in_dim(cells, cells.shape[dim] - width, cells.shape[dim], axis=dim)
        cells = jnp.concatenate(
            [
                lax.ppermute(tail, axis, [(i, (i + 1) % count) for i in range(ends)]),
                cells,
                lax.ppermute(head, axis, [((i + 1) % count, i) for i in range(ends)]),
            ],
            axis=dim,
        )
    return cells


def forward_arrange(cube):
    depth, rows_t, cols_t, inputs, outputs = cube.shape
    return cube.transpose(0, 1, 3, 2, 4).reshape(9, inputs, 3 * outputs)


def backward_arrange(cube):
    depth, rows_t, cols_t, inputs, outputs = cube.shape
    return cube.transpose(0, 1, 4, 2, 3).reshape(9, outputs, 3 * inputs)


def forward_sum(window, cube, row_total, col_total):
    width = window.shape[-1]
    padded_cols = window.shape[2]
    slots = cube.shape[-1]
    totals = []
    for col_tap in range(3):
        total = None
        for depth_tap in range(3):
            for row_tap in range(3):
                slab = window[depth_tap, row_tap : row_tap + row_total].reshape(
                    row_total * padded_cols, width
                )
                product = jnp.dot(
                    slab, cube[depth_tap, row_tap, col_tap], preferred_element_type=jnp.float32
                )
                total = product if total is None else total + product
        totals.append(total.reshape(row_total, padded_cols, slots))
    return (
        totals[0][:, 0:col_total] + totals[1][:, 1 : col_total + 1] + totals[2][:, 2 : col_total + 2]
    )


def backward_sum(window, arranged, row_total, col_total):
    width = window.shape[-1]
    slots = arranged.shape[-1] // 3
    total = None
    for depth_tap in range(3):
        for row_tap in range(3):
            slab = window[2 - depth_tap, 2 - row_tap : 2 - row_tap + row_total].reshape(
                row_total * window.shape[2], width
            )
            product = jnp.dot(
                slab, arranged[3 * depth_tap + row_tap], preferred_element_type=jnp.float32
            )
            total = product if total is None else total + product
    total = total.reshape(row_total, window.shape[2], 3, slots)
    return (
        total[:, 2 : col_total + 2, 0] + total[:, 1 : col_total + 1, 1] + total[:, 0:col_total, 2]
    )


def pair_count(tap_rows, share_rows, pair_rows, parts):
    most = 1
    for index in range(parts):
        first = index * share_rows
        last = first + share_rows - 1
        most = max(most, last // pair_rows - first // pair_rows + 1)
    return most


def block_weight_grad(framed, cot_all, frame_index, share_rows, channels):
    frame_total, row_total, col_total, slots = cot_all.shape
    padded_cols = framed.shape[2]
    pair_rows = 3 * channels
    tap_rows = 27 * channels
    flat_count = frame_total * row_total * padded_cols
    shifted = jnp.concatenate(
        [
            jnp.pad(
                cot_all,
                ((0, 0), (0, 0), (col_tap, padded_cols - col_total - col_tap), (0, 0)),
            )
            for col_tap in range(3)
        ],
        axis=-1,
    ).reshape(flat_count, 3 * slots)
    first_row = frame_index * share_rows
    first_pair = first_row // pair_rows
    count = pair_count(tap_rows, share_rows, pair_rows, tap_rows // share_rows)
    pieces = []
    for step in range(count):
        pair = jnp.minimum(first_pair + step, 8)
        depth_tap = pair // 3
        row_tap = pair % 3
        slab = lax.dynamic_slice(
            framed,
            (depth_tap, row_tap, 0, 0),
            (frame_total, row_total, padded_cols, channels),
        ).reshape(flat_count, channels)
        product = lax.dot_general(
            slab, shifted, (((0,), (0,)), ((), ())), preferred_element_type=jnp.float32
        )
        pieces.append(product.reshape(channels, 3, slots).transpose(1, 0, 2).reshape(pair_rows, slots))
    stacked = jnp.concatenate(pieces, axis=0)
    return lax.dynamic_slice_in_dim(stacked, first_row - first_pair * pair_rows, share_rows, 0)


def local(latents, gain, bias, weight, cotangent):
    frame_count, row_count, col_count, channels = latents.shape
    latent_wide = latents.astype(jnp.float32)
    root_mean = jnp.sqrt(jnp.mean(latent_wide * latent_wide, axis=-1, keepdims=True) + 1e-06)
    normed = latent_wide / root_mean * gain
    hidden = jax.nn.silu(normed).astype(jnp.bfloat16)
    height_count = lax.axis_size("height")
    frame_devices = lax.axis_size("tm")
    frame_index = lax.axis_index("tm")
    row_index = lax.axis_index("height")
    total_rows = row_count * height_count
    total_frames = frame_count * frame_devices
    tap_rows = 27 * channels
    share_rows = tap_rows // frame_devices
    padded_cols = -(-(col_count + 2) // 8) * 8
    right_pad = padded_cols - col_count - 1
    inverse_root = 1.0 / math.sqrt(total_frames * total_rows * col_count)
    weight_cube = weight.reshape(3, 3, 3, channels, channels)

    both_frames = lax.all_gather(
        jnp.concatenate([hidden, cotangent], axis=-1), "tm", axis=0, tiled=True
    )
    hidden_all = lax.all_gather(both_frames[..., :channels], "height", axis=1, tiled=True)
    framed = jnp.pad(hidden_all, ((2, 0), (1, 1), (1, right_pad), (0, 0)))

    cot_frames = both_frames[..., channels:]
    cot_all = lax.all_to_all(cot_frames, "height", split_axis=3, concat_axis=1, tiled=True)

    window = lax.dynamic_slice(
        framed,
        (frame_index * frame_count, row_index * row_count, 0, 0),
        (frame_count + 2, row_count + 2, padded_cols, channels),
    )
    conv_out = forward_sum(window, weight_cube, row_count, col_count).reshape(
        frame_count, row_count, col_count, channels
    )
    output = (latent_wide + conv_out + bias).astype(jnp.bfloat16)

    weight_grad = block_weight_grad(framed, cot_all, frame_index, share_rows, channels) * inverse_root

    cot_future = lax.dynamic_slice_in_dim(
        jnp.pad(cot_frames, ((0, 2), (0, 0), (0, 0), (0, 0))), frame_index * frame_count, 3, 0
    )
    cotangent_edged = padded(cot_future, (("height", 1),), 1)
    future_block = jnp.pad(cotangent_edged, ((0, 0), (0, 0), (1, right_pad), (0, 0)))
    hidden_grad = backward_sum(
        future_block, backward_arrange(weight_cube), row_count, col_count
    ).reshape(frame_count, row_count, col_count, channels)
    sigmoid_pre = jax.nn.sigmoid(normed)
    normed_grad = hidden_grad * sigmoid_pre * (1.0 + normed * (1.0 - sigmoid_pre))
    scaled_grad = normed_grad * gain
    unit_latent = latent_wide / root_mean
    inner = jnp.mean(scaled_grad * unit_latent, axis=-1, keepdims=True)
    latent_grad = (
        cotangent.astype(jnp.float32) + (scaled_grad - unit_latent * inner) / root_mean
    ).astype(jnp.bfloat16)
    return (output, latent_grad, weight_grad)


def solution(mesh):
    placed = (
        P(("grp", "tm"), "height", None, None),
        P(),
        P(),
        P(),
        P(("grp", "tm"), "height", None, None),
    )
    return jax.shard_map(
        local,
        mesh=mesh,
        in_specs=placed,
        out_specs=(
            P(("grp", "tm"), "height", None, None),
            P(("grp", "tm"), "height", None, None),
            P(("grp", "tm"), "height"),
        ),
        check_vma=False,
    )
```

```python
import math

import jax
import jax.numpy as jnp
from jax import lax
from jax.sharding import PartitionSpec as P


def shifted_2(value, axis, by):
    devices = lax.axis_size(axis)
    pairs = [(i, i + by) for i in range(devices) if 0 <= i + by < devices]
    return lax.ppermute(value, axis, pairs)


def padded(cells, sides, width):
    for axis, dim in sides:
        count = lax.axis_size(axis)
        ends = count - 1
        head = lax.slice_in_dim(cells, 0, width, axis=dim)
        tail = lax.slice_in_dim(cells, cells.shape[dim] - width, cells.shape[dim], axis=dim)
        cells = jnp.concatenate(
            [
                lax.ppermute(tail, axis, [(i, (i + 1) % count) for i in range(ends)]),
                cells,
                lax.ppermute(head, axis, [((i + 1) % count, i) for i in range(ends)]),
            ],
            axis=dim,
        )
    return cells


def forward_arrange(cube):
    depth, rows_t, cols_t, inputs, outputs = cube.shape
    return cube.transpose(0, 1, 3, 2, 4).reshape(9, inputs, 3 * outputs)


def backward_arrange(cube):
    depth, rows_t, cols_t, inputs, outputs = cube.shape
    return cube.transpose(0, 1, 4, 2, 3).reshape(9, outputs, 3 * inputs)


def forward_sum(window, weight, row_total, col_total):
    pieces = []
    for depth_tap in range(3):
        for row_tap in range(3):
            for col_tap in range(3):
                pieces.append(
                    window[depth_tap, row_tap : row_tap + row_total, col_tap : col_tap + col_total]
                )
    patch = jnp.concatenate(pieces, axis=-1).reshape(row_total * col_total, weight.shape[0])
    return jnp.dot(patch, weight, preferred_element_type=jnp.float32)


def backward_sum(window, arranged, row_total, col_total):
    width = window.shape[-1]
    slots = arranged.shape[-1] // 3
    total = None
    for depth_tap in range(3):
        for row_tap in range(3):
            slab = window[2 - depth_tap, 2 - row_tap : 2 - row_tap + row_total].reshape(
                row_total * window.shape[2], width
            )
            product = jnp.dot(
                slab, arranged[3 * depth_tap + row_tap], preferred_element_type=jnp.float32
            )
            total = product if total is None else total + product
    total = total.reshape(row_total, window.shape[2], 3, slots)
    return (
        total[:, 2 : col_total + 2, 0] + total[:, 1 : col_total + 1, 1] + total[:, 0:col_total, 2]
    )


def pair_count(tap_rows, share_rows, pair_rows, parts):
    most = 1
    for index in range(parts):
        first = index * share_rows
        last = first + share_rows - 1
        most = max(most, last // pair_rows - first // pair_rows + 1)
    return most


def block_weight_grad(framed, cot_all, frame_index, share_rows, channels):
    frame_total, row_total, col_total, slots = cot_all.shape
    padded_cols = framed.shape[2]
    pair_rows = 3 * channels
    tap_rows = 27 * channels
    flat_count = frame_total * row_total * padded_cols
    shifted = jnp.concatenate(
        [
            jnp.pad(
                cot_all,
                ((0, 0), (0, 0), (col_tap, padded_cols - col_total - col_tap), (0, 0)),
            )
            for col_tap in range(3)
        ],
        axis=-1,
    ).reshape(flat_count, 3 * slots)
    first_row = frame_index * share_rows
    first_pair = first_row // pair_rows
    count = pair_count(tap_rows, share_rows, pair_rows, tap_rows // share_rows)
    pieces = []
    for step in range(count):
        pair = jnp.minimum(first_pair + step, 8)
        depth_tap = pair // 3
        row_tap = pair % 3
        slab = lax.dynamic_slice(
            framed,
            (depth_tap, row_tap, 0, 0),
            (frame_total, row_total, padded_cols, channels),
        ).reshape(flat_count, channels)
        product = lax.dot_general(
            slab, shifted, (((0,), (0,)), ((), ())), preferred_element_type=jnp.float32
        )
        pieces.append(product.reshape(channels, 3, slots).transpose(1, 0, 2).reshape(pair_rows, slots))
    stacked = jnp.concatenate(pieces, axis=0)
    return lax.dynamic_slice_in_dim(stacked, first_row - first_pair * pair_rows, share_rows, 0)


def gather_rows(own, height_count):
    frame_total, row_count, col_count, channels = own.shape
    height_index = lax.axis_index("height")
    core = height_index % 2
    chip = height_index // 2
    chips = height_count // 2
    first = core == 0
    sibling = [(i, i ^ 1) for i in range(height_count)]
    twin = lax.ppermute(own, "height", sibling)
    chip_rows = jnp.where(
        first, jnp.concatenate([own, twin], axis=1), jnp.concatenate([twin, own], axis=1)
    )
    if chips == 1:
        return chip_rows
    half = col_count // 2
    mine = lax.dynamic_slice_in_dim(chip_rows, core * half, half, axis=2)
    got = jnp.concatenate(
        [
            lax.ppermute(
                mine, "height", [(i, (i + 2 * step) % height_count) for i in range(height_count)]
            )
            for step in range(1, chips)
        ],
        axis=1,
    )
    other = lax.ppermute(got, "height", sibling)
    full = jnp.where(
        first, jnp.concatenate([got, other], axis=2), jnp.concatenate([other, got], axis=2)
    )
    relative = jnp.concatenate([chip_rows, full], axis=1)
    block = 2 * row_count
    reverse = jnp.concatenate(
        [relative[:, step * block : (step + 1) * block] for step in reversed(range(chips))], axis=1
    )
    return jnp.roll(reverse, (chip + 1) * block, axis=1)


def local(latents, gain, bias, weight, cotangent):
    frame_count, row_count, col_count, channels = latents.shape
    latent_wide = latents.astype(jnp.float32)
    root_mean = jnp.sqrt(jnp.mean(latent_wide * latent_wide, axis=-1, keepdims=True) + 1e-06)
    normed = latent_wide / root_mean * gain
    hidden = jax.nn.silu(normed).astype(jnp.bfloat16)
    height_count = lax.axis_size("height")
    frame_devices = lax.axis_size("tm")
    frame_index = lax.axis_index("tm")
    row_index = lax.axis_index("height")
    total_rows = row_count * height_count
    total_frames = frame_count * frame_devices
    tap_rows = 27 * channels
    share_rows = tap_rows // frame_devices
    padded_cols = -(-(col_count + 2) // 8) * 8
    right_pad = padded_cols - col_count - 1
    inverse_root = 1.0 / math.sqrt(total_frames * total_rows * col_count)
    weight_cube = weight.reshape(3, 3, 3, channels, channels)

    both_frames = lax.all_gather(
        jnp.concatenate([hidden, cotangent], axis=-1), "tm", axis=0, tiled=True
    )
    hidden_all = gather_rows(both_frames[..., :channels], height_count)
    framed = jnp.pad(hidden_all, ((2, 0), (1, 1), (1, right_pad), (0, 0)))

    cot_frames = both_frames[..., channels:]
    cot_all = lax.all_to_all(cot_frames, "height", split_axis=3, concat_axis=1, tiled=True)

    window = lax.dynamic_slice(
        framed,
        (frame_index * frame_count, row_index * row_count, 0, 0),
        (frame_count + 2, row_count + 2, padded_cols, channels),
    )
    conv_out = forward_sum(window, weight, row_count, col_count).reshape(
        frame_count, row_count, col_count, channels
    )
    output = (latent_wide + conv_out + bias).astype(jnp.bfloat16)

    weight_grad = block_weight_grad(framed, cot_all, frame_index, share_rows, channels) * inverse_root

    cot_future = lax.dynamic_slice_in_dim(
        jnp.pad(cot_frames, ((0, 2), (0, 0), (0, 0), (0, 0))), frame_index * frame_count, 3, 0
    )
    cotangent_edged = padded(cot_future, (("height", 1),), 1)
    future_block = jnp.pad(cotangent_edged, ((0, 0), (0, 0), (1, right_pad), (0, 0)))
    hidden_grad = backward_sum(
        future_block, backward_arrange(weight_cube), row_count, col_count
    ).reshape(frame_count, row_count, col_count, channels)
    sigmoid_pre = jax.nn.sigmoid(normed)
    normed_grad = hidden_grad * sigmoid_pre * (1.0 + normed * (1.0 - sigmoid_pre))
    scaled_grad = normed_grad * gain
    unit_latent = latent_wide / root_mean
    inner = jnp.mean(scaled_grad * unit_latent, axis=-1, keepdims=True)
    latent_grad = (
        cotangent.astype(jnp.float32) + (scaled_grad - unit_latent * inner) / root_mean
    ).astype(jnp.bfloat16)
    return (output, latent_grad, weight_grad)


def solution(mesh):
    placed = (
        P(("grp", "tm"), "height", None, None),
        P(),
        P(),
        P(),
        P(("grp", "tm"), "height", None, None),
    )
    return jax.shard_map(
        local,
        mesh=mesh,
        in_specs=placed,
        out_specs=(
            P(("grp", "tm"), "height", None, None),
            P(("grp", "tm"), "height", None, None),
            P(("grp", "tm"), "height"),
        ),
        check_vma=False,
    )
```

```python
import math

import jax
import jax.numpy as jnp
from jax import lax
from jax.sharding import PartitionSpec as P


def shifted_2(value, axis, by):
    devices = lax.axis_size(axis)
    pairs = [(i, i + by) for i in range(devices) if 0 <= i + by < devices]
    return lax.ppermute(value, axis, pairs)


def padded(cells, sides, width):
    for axis, dim in sides:
        count = lax.axis_size(axis)
        ends = count - 1
        head = lax.slice_in_dim(cells, 0, width, axis=dim)
        tail = lax.slice_in_dim(cells, cells.shape[dim] - width, cells.shape[dim], axis=dim)
        cells = jnp.concatenate(
            [
                lax.ppermute(tail, axis, [(i, (i + 1) % count) for i in range(ends)]),
                cells,
                lax.ppermute(head, axis, [((i + 1) % count, i) for i in range(ends)]),
            ],
            axis=dim,
        )
    return cells


def forward_arrange(cube):
    depth, rows_t, cols_t, inputs, outputs = cube.shape
    return cube.transpose(0, 1, 3, 2, 4).reshape(9, inputs, 3 * outputs)


def backward_arrange(cube):
    depth, rows_t, cols_t, inputs, outputs = cube.shape
    return cube.transpose(0, 1, 4, 2, 3).reshape(9, outputs, 3 * inputs)


def forward_sum(window, weight, row_total, col_total):
    pieces = []
    for depth_tap in range(3):
        for row_tap in range(3):
            for col_tap in range(3):
                pieces.append(
                    window[depth_tap, row_tap : row_tap + row_total, col_tap : col_tap + col_total]
                )
    patch = jnp.concatenate(pieces, axis=-1).reshape(row_total * col_total, weight.shape[0])
    return jnp.dot(patch, weight, preferred_element_type=jnp.float32)


def backward_sum(window, arranged, row_total, col_total):
    width = window.shape[-1]
    slots = arranged.shape[-1] // 3
    total = None
    for depth_tap in range(3):
        for row_tap in range(3):
            slab = window[2 - depth_tap, 2 - row_tap : 2 - row_tap + row_total].reshape(
                row_total * window.shape[2], width
            )
            product = jnp.dot(
                slab, arranged[3 * depth_tap + row_tap], preferred_element_type=jnp.float32
            )
            total = product if total is None else total + product
    total = total.reshape(row_total, window.shape[2], 3, slots)
    return (
        total[:, 2 : col_total + 2, 0] + total[:, 1 : col_total + 1, 1] + total[:, 0:col_total, 2]
    )


def pair_count(tap_rows, share_rows, pair_rows, parts):
    most = 1
    for index in range(parts):
        first = index * share_rows
        last = first + share_rows - 1
        most = max(most, last // pair_rows - first // pair_rows + 1)
    return most


def block_weight_grad(framed, cot_all, frame_index, share_rows, channels):
    frame_total, row_total, col_total, slots = cot_all.shape
    padded_cols = framed.shape[2]
    pair_rows = 3 * channels
    tap_rows = 27 * channels
    flat_count = frame_total * row_total * padded_cols
    shifted = jnp.concatenate(
        [
            jnp.pad(
                cot_all,
                ((0, 0), (0, 0), (col_tap, padded_cols - col_total - col_tap), (0, 0)),
            )
            for col_tap in range(3)
        ],
        axis=-1,
    ).reshape(flat_count, 3 * slots)
    first_row = frame_index * share_rows
    first_pair = first_row // pair_rows
    count = pair_count(tap_rows, share_rows, pair_rows, tap_rows // share_rows)
    pieces = []
    for step in range(count):
        pair = jnp.minimum(first_pair + step, 8)
        depth_tap = pair // 3
        row_tap = pair % 3
        slab = lax.dynamic_slice(
            framed,
            (depth_tap, row_tap, 0, 0),
            (frame_total, row_total, padded_cols, channels),
        ).reshape(flat_count, channels)
        product = lax.dot_general(
            slab, shifted, (((0,), (0,)), ((), ())), preferred_element_type=jnp.float32
        )
        pieces.append(product.reshape(channels, 3, slots).transpose(1, 0, 2).reshape(pair_rows, slots))
    stacked = jnp.concatenate(pieces, axis=0)
    return lax.dynamic_slice_in_dim(stacked, first_row - first_pair * pair_rows, share_rows, 0)


def gather_rows(own, height_count):
    frame_total, row_count, col_count, channels = own.shape
    height_index = lax.axis_index("height")
    core = height_index % 2
    chip = height_index // 2
    chips = height_count // 2
    first = core == 0
    sibling = [(i, i ^ 1) for i in range(height_count)]
    mine = [own] + [
        lax.ppermute(
            own, "height", [(i, (i + 2 * step) % height_count) for i in range(height_count)]
        )
        for step in range(1, chips)
    ]
    stacked = jnp.concatenate(mine, axis=1)
    twins = lax.ppermute(stacked, "height", sibling)
    block = 2 * row_count
    relative = []
    for step in reversed(range(chips)):
        ours = stacked[:, step * row_count : (step + 1) * row_count]
        theirs = twins[:, step * row_count : (step + 1) * row_count]
        relative.append(
            jnp.where(
                first,
                jnp.concatenate([ours, theirs], axis=1),
                jnp.concatenate([theirs, ours], axis=1),
            )
        )
    return jnp.roll(jnp.concatenate(relative, axis=1), (chip + 1) * block, axis=1)


def local(latents, gain, bias, weight, cotangent):
    frame_count, row_count, col_count, channels = latents.shape
    latent_wide = latents.astype(jnp.float32)
    root_mean = jnp.sqrt(jnp.mean(latent_wide * latent_wide, axis=-1, keepdims=True) + 1e-06)
    normed = latent_wide / root_mean * gain
    hidden = jax.nn.silu(normed).astype(jnp.bfloat16)
    height_count = lax.axis_size("height")
    frame_devices = lax.axis_size("tm")
    frame_index = lax.axis_index("tm")
    row_index = lax.axis_index("height")
    total_rows = row_count * height_count
    total_frames = frame_count * frame_devices
    tap_rows = 27 * channels
    share_rows = tap_rows // frame_devices
    padded_cols = -(-(col_count + 2) // 8) * 8
    right_pad = padded_cols - col_count - 1
    inverse_root = 1.0 / math.sqrt(total_frames * total_rows * col_count)
    weight_cube = weight.reshape(3, 3, 3, channels, channels)

    both_frames = lax.all_gather(
        jnp.concatenate([hidden, cotangent], axis=-1), "tm", axis=0, tiled=True
    )
    hidden_all = gather_rows(both_frames[..., :channels], height_count)
    framed = jnp.pad(hidden_all, ((2, 0), (1, 1), (1, right_pad), (0, 0)))

    cot_frames = both_frames[..., channels:]
    cot_all = lax.all_to_all(cot_frames, "height", split_axis=3, concat_axis=1, tiled=True)

    window = lax.dynamic_slice(
        framed,
        (frame_index * frame_count, row_index * row_count, 0, 0),
        (frame_count + 2, row_count + 2, padded_cols, channels),
    )
    conv_out = forward_sum(window, weight, row_count, col_count).reshape(
        frame_count, row_count, col_count, channels
    )
    output = (latent_wide + conv_out + bias).astype(jnp.bfloat16)

    weight_grad = block_weight_grad(framed, cot_all, frame_index, share_rows, channels) * inverse_root

    cot_future = lax.dynamic_slice_in_dim(
        jnp.pad(cot_frames, ((0, 2), (0, 0), (0, 0), (0, 0))), frame_index * frame_count, 3, 0
    )
    cotangent_edged = padded(cot_future, (("height", 1),), 1)
    future_block = jnp.pad(cotangent_edged, ((0, 0), (0, 0), (1, right_pad), (0, 0)))
    hidden_grad = backward_sum(
        future_block, backward_arrange(weight_cube), row_count, col_count
    ).reshape(frame_count, row_count, col_count, channels)
    sigmoid_pre = jax.nn.sigmoid(normed)
    normed_grad = hidden_grad * sigmoid_pre * (1.0 + normed * (1.0 - sigmoid_pre))
    scaled_grad = normed_grad * gain
    unit_latent = latent_wide / root_mean
    inner = jnp.mean(scaled_grad * unit_latent, axis=-1, keepdims=True)
    latent_grad = (
        cotangent.astype(jnp.float32) + (scaled_grad - unit_latent * inner) / root_mean
    ).astype(jnp.bfloat16)
    return (output, latent_grad, weight_grad)


def solution(mesh):
    placed = (
        P(("grp", "tm"), "height", None, None),
        P(),
        P(),
        P(),
        P(("grp", "tm"), "height", None, None),
    )
    return jax.shard_map(
        local,
        mesh=mesh,
        in_specs=placed,
        out_specs=(
            P(("grp", "tm"), "height", None, None),
            P(("grp", "tm"), "height", None, None),
            P(("grp", "tm"), "height"),
        ),
        check_vma=False,
    )
```

```python
import math

import jax
import jax.numpy as jnp
from jax import lax
from jax.sharding import PartitionSpec as P


def shifted_2(value, axis, by):
    devices = lax.axis_size(axis)
    pairs = [(i, i + by) for i in range(devices) if 0 <= i + by < devices]
    return lax.ppermute(value, axis, pairs)


def padded(cells, sides, width):
    for axis, dim in sides:
        count = lax.axis_size(axis)
        ends = count - 1
        head = lax.slice_in_dim(cells, 0, width, axis=dim)
        tail = lax.slice_in_dim(cells, cells.shape[dim] - width, cells.shape[dim], axis=dim)
        cells = jnp.concatenate(
            [
                lax.ppermute(tail, axis, [(i, (i + 1) % count) for i in range(ends)]),
                cells,
                lax.ppermute(head, axis, [((i + 1) % count, i) for i in range(ends)]),
            ],
            axis=dim,
        )
    return cells


def forward_arrange(cube):
    depth, rows_t, cols_t, inputs, outputs = cube.shape
    return cube.transpose(0, 1, 3, 2, 4).reshape(9, inputs, 3 * outputs)


def backward_arrange(cube):
    depth, rows_t, cols_t, inputs, outputs = cube.shape
    return cube.transpose(0, 1, 4, 2, 3).reshape(9, outputs, 3 * inputs)


def forward_conv(window, cube, row_total, col_total):
    window = window[:, :, : col_total + 2]
    result = lax.conv_general_dilated(
        window[None],
        cube,
        (1, 1, 1),
        "VALID",
        dimension_numbers=("NDHWC", "DHWIO", "NDHWC"),
        preferred_element_type=jnp.float32,
    )
    return result[0, 0]


def backward_conv(window, cube, row_total, col_total):
    window = window[:, :, : col_total + 2]
    result = lax.conv_general_dilated(
        window[None],
        jnp.flip(cube, (0, 1, 2)),
        (1, 1, 1),
        "VALID",
        dimension_numbers=("NDHWC", "DHWOI", "NDHWC"),
        preferred_element_type=jnp.float32,
    )
    return result[0, 0]


def pair_count(tap_rows, share_rows, pair_rows, parts):
    most = 1
    for index in range(parts):
        first = index * share_rows
        last = first + share_rows - 1
        most = max(most, last // pair_rows - first // pair_rows + 1)
    return most


def block_weight_grad(framed, cot_all, frame_index, share_rows, channels):
    frame_total, row_total, col_total, slots = cot_all.shape
    padded_cols = framed.shape[2]
    pair_rows = 3 * channels
    tap_rows = 27 * channels
    flat_count = frame_total * row_total * padded_cols
    shifted = jnp.concatenate(
        [
            jnp.pad(
                cot_all,
                ((0, 0), (0, 0), (col_tap, padded_cols - col_total - col_tap), (0, 0)),
            )
            for col_tap in range(3)
        ],
        axis=-1,
    ).reshape(flat_count, 3 * slots)
    first_row = frame_index * share_rows
    first_pair = first_row // pair_rows
    count = pair_count(tap_rows, share_rows, pair_rows, tap_rows // share_rows)
    pieces = []
    for step in range(count):
        pair = jnp.minimum(first_pair + step, 8)
        depth_tap = pair // 3
        row_tap = pair % 3
        slab = lax.dynamic_slice(
            framed,
            (depth_tap, row_tap, 0, 0),
            (frame_total, row_total, padded_cols, channels),
        ).reshape(flat_count, channels)
        product = lax.dot_general(
            slab, shifted, (((0,), (0,)), ((), ())), preferred_element_type=jnp.float32
        )
        pieces.append(product.reshape(channels, 3, slots).transpose(1, 0, 2).reshape(pair_rows, slots))
    stacked = jnp.concatenate(pieces, axis=0)
    return lax.dynamic_slice_in_dim(stacked, first_row - first_pair * pair_rows, share_rows, 0)


def gather_rows(own, height_count):
    frame_total, row_count, col_count, channels = own.shape
    height_index = lax.axis_index("height")
    core = height_index % 2
    chip = height_index // 2
    chips = height_count // 2
    first = core == 0
    sibling = [(i, i ^ 1) for i in range(height_count)]
    twin = lax.ppermute(own, "height", sibling)
    chip_rows = jnp.where(
        first, jnp.concatenate([own, twin], axis=1), jnp.concatenate([twin, own], axis=1)
    )
    if chips == 1:
        return chip_rows
    half = col_count // 2
    mine = lax.dynamic_slice_in_dim(chip_rows, core * half, half, axis=2)
    got = jnp.concatenate(
        [
            lax.ppermute(
                mine, "height", [(i, (i + 2 * step) % height_count) for i in range(height_count)]
            )
            for step in range(1, chips)
        ],
        axis=1,
    )
    other = lax.ppermute(got, "height", sibling)
    full = jnp.where(
        first, jnp.concatenate([got, other], axis=2), jnp.concatenate([other, got], axis=2)
    )
    relative = jnp.concatenate([chip_rows, full], axis=1)
    block = 2 * row_count
    reverse = jnp.concatenate(
        [relative[:, step * block : (step + 1) * block] for step in reversed(range(chips))], axis=1
    )
    return jnp.roll(reverse, (chip + 1) * block, axis=1)


def local(latents, gain, bias, weight, cotangent):
    frame_count, row_count, col_count, channels = latents.shape
    latent_wide = latents.astype(jnp.float32)
    root_mean = jnp.sqrt(jnp.mean(latent_wide * latent_wide, axis=-1, keepdims=True) + 1e-06)
    normed = latent_wide / root_mean * gain
    hidden = jax.nn.silu(normed).astype(jnp.bfloat16)
    height_count = lax.axis_size("height")
    frame_devices = lax.axis_size("tm")
    frame_index = lax.axis_index("tm")
    row_index = lax.axis_index("height")
    total_rows = row_count * height_count
    total_frames = frame_count * frame_devices
    tap_rows = 27 * channels
    share_rows = tap_rows // frame_devices
    padded_cols = -(-(col_count + 2) // 8) * 8
    right_pad = padded_cols - col_count - 1
    inverse_root = 1.0 / math.sqrt(total_frames * total_rows * col_count)
    weight_cube = weight.reshape(3, 3, 3, channels, channels)

    both_frames = lax.all_gather(
        jnp.concatenate([hidden, cotangent], axis=-1), "tm", axis=0, tiled=True
    )
    hidden_all = gather_rows(both_frames[..., :channels], height_count)
    framed = jnp.pad(hidden_all, ((2, 0), (1, 1), (1, right_pad), (0, 0)))

    cot_frames = both_frames[..., channels:]
    cot_all = lax.all_to_all(cot_frames, "height", split_axis=3, concat_axis=1, tiled=True)

    window = lax.dynamic_slice(
        framed,
        (frame_index * frame_count, row_index * row_count, 0, 0),
        (frame_count + 2, row_count + 2, padded_cols, channels),
    )
    conv_out = forward_conv(window, weight_cube, row_count, col_count).reshape(
        frame_count, row_count, col_count, channels
    )
    output = (latent_wide + conv_out + bias).astype(jnp.bfloat16)

    weight_grad = block_weight_grad(framed, cot_all, frame_index, share_rows, channels) * inverse_root

    cot_future = lax.dynamic_slice_in_dim(
        jnp.pad(cot_frames, ((0, 2), (0, 0), (0, 0), (0, 0))), frame_index * frame_count, 3, 0
    )
    cotangent_edged = padded(cot_future, (("height", 1),), 1)
    future_block = jnp.pad(cotangent_edged, ((0, 0), (0, 0), (1, right_pad), (0, 0)))
    hidden_grad = backward_conv(future_block, weight_cube, row_count, col_count).reshape(frame_count, row_count, col_count, channels)
    sigmoid_pre = jax.nn.sigmoid(normed)
    normed_grad = hidden_grad * sigmoid_pre * (1.0 + normed * (1.0 - sigmoid_pre))
    scaled_grad = normed_grad * gain
    unit_latent = latent_wide / root_mean
    inner = jnp.mean(scaled_grad * unit_latent, axis=-1, keepdims=True)
    latent_grad = (
        cotangent.astype(jnp.float32) + (scaled_grad - unit_latent * inner) / root_mean
    ).astype(jnp.bfloat16)
    return (output, latent_grad, weight_grad)


def solution(mesh):
    placed = (
        P(("grp", "tm"), "height", None, None),
        P(),
        P(),
        P(),
        P(("grp", "tm"), "height", None, None),
    )
    return jax.shard_map(
        local,
        mesh=mesh,
        in_specs=placed,
        out_specs=(
            P(("grp", "tm"), "height", None, None),
            P(("grp", "tm"), "height", None, None),
            P(("grp", "tm"), "height"),
        ),
        check_vma=False,
    )
```

```python
import math

import jax
import jax.numpy as jnp
from jax import lax
from jax.sharding import PartitionSpec as P


def shifted_2(value, axis, by):
    devices = lax.axis_size(axis)
    pairs = [(i, i + by) for i in range(devices) if 0 <= i + by < devices]
    return lax.ppermute(value, axis, pairs)


def padded(cells, sides, width):
    for axis, dim in sides:
        count = lax.axis_size(axis)
        ends = count - 1
        head = lax.slice_in_dim(cells, 0, width, axis=dim)
        tail = lax.slice_in_dim(cells, cells.shape[dim] - width, cells.shape[dim], axis=dim)
        cells = jnp.concatenate(
            [
                lax.ppermute(tail, axis, [(i, (i + 1) % count) for i in range(ends)]),
                cells,
                lax.ppermute(head, axis, [((i + 1) % count, i) for i in range(ends)]),
            ],
            axis=dim,
        )
    return cells


def forward_arrange(cube):
    depth, rows_t, cols_t, inputs, outputs = cube.shape
    return cube.transpose(0, 1, 3, 2, 4).reshape(9, inputs, 3 * outputs)


def backward_arrange(cube):
    depth, rows_t, cols_t, inputs, outputs = cube.shape
    return cube.transpose(0, 1, 4, 2, 3).reshape(9, outputs, 3 * inputs)


def forward_conv(window, cube, row_total, col_total):
    window = window[:, :, : col_total + 2]
    result = lax.conv_general_dilated(
        window[None],
        cube,
        (1, 1, 1),
        "VALID",
        dimension_numbers=("NDHWC", "DHWIO", "NDHWC"),
        preferred_element_type=jnp.float32,
    )
    return result[0, 0]


def backward_conv(window, cube, row_total, col_total):
    window = window[:, :, : col_total + 2]
    result = lax.conv_general_dilated(
        window[None],
        jnp.flip(cube, (0, 1, 2)),
        (1, 1, 1),
        "VALID",
        dimension_numbers=("NDHWC", "DHWOI", "NDHWC"),
        preferred_element_type=jnp.float32,
    )
    return result[0, 0]


def pair_count(tap_rows, share_rows, pair_rows, parts):
    most = 1
    for index in range(parts):
        first = index * share_rows
        last = first + share_rows - 1
        most = max(most, last // pair_rows - first // pair_rows + 1)
    return most


def block_weight_grad(framed, cot_all, frame_index, share_rows, channels):
    frame_total, row_total, col_total, slots = cot_all.shape
    padded_cols = framed.shape[2]
    pair_rows = 3 * channels
    tap_rows = 27 * channels
    flat_count = frame_total * row_total * padded_cols
    shifted = jnp.concatenate(
        [
            jnp.pad(
                cot_all,
                ((0, 0), (0, 0), (col_tap, padded_cols - col_total - col_tap), (0, 0)),
            )
            for col_tap in range(3)
        ],
        axis=-1,
    ).reshape(flat_count, 3 * slots)
    first_row = frame_index * share_rows
    first_pair = first_row // pair_rows
    count = pair_count(tap_rows, share_rows, pair_rows, tap_rows // share_rows)
    pieces = []
    for step in range(count):
        pair = jnp.minimum(first_pair + step, 8)
        depth_tap = pair // 3
        row_tap = pair % 3
        slab = lax.dynamic_slice(
            framed,
            (depth_tap, row_tap, 0, 0),
            (frame_total, row_total, padded_cols, channels),
        ).reshape(flat_count, channels)
        product = lax.dot_general(
            slab, shifted, (((0,), (0,)), ((), ())), preferred_element_type=jnp.float32
        )
        pieces.append(product.reshape(channels, 3, slots).transpose(1, 0, 2).reshape(pair_rows, slots))
    stacked = jnp.concatenate(pieces, axis=0)
    return lax.dynamic_slice_in_dim(stacked, first_row - first_pair * pair_rows, share_rows, 0)


def gather_rows(own, height_count):
    frame_total, row_count, col_count, channels = own.shape
    height_index = lax.axis_index("height")
    core = height_index % 2
    chip = height_index // 2
    chips = height_count // 2
    first = core == 0
    sibling = [(i, i ^ 1) for i in range(height_count)]
    mine = [own] + [
        lax.ppermute(
            own, "height", [(i, (i + 2 * step) % height_count) for i in range(height_count)]
        )
        for step in range(1, chips)
    ]
    stacked = jnp.concatenate(mine, axis=1)
    twins = lax.ppermute(stacked, "height", sibling)
    block = 2 * row_count
    relative = []
    for step in reversed(range(chips)):
        ours = stacked[:, step * row_count : (step + 1) * row_count]
        theirs = twins[:, step * row_count : (step + 1) * row_count]
        relative.append(
            jnp.where(
                first,
                jnp.concatenate([ours, theirs], axis=1),
                jnp.concatenate([theirs, ours], axis=1),
            )
        )
    return jnp.roll(jnp.concatenate(relative, axis=1), (chip + 1) * block, axis=1)


def local(latents, gain, bias, weight, cotangent):
    frame_count, row_count, col_count, channels = latents.shape
    latent_wide = latents.astype(jnp.float32)
    root_mean = jnp.sqrt(jnp.mean(latent_wide * latent_wide, axis=-1, keepdims=True) + 1e-06)
    normed = latent_wide / root_mean * gain
    hidden = jax.nn.silu(normed).astype(jnp.bfloat16)
    height_count = lax.axis_size("height")
    frame_devices = lax.axis_size("tm")
    frame_index = lax.axis_index("tm")
    row_index = lax.axis_index("height")
    total_rows = row_count * height_count
    total_frames = frame_count * frame_devices
    tap_rows = 27 * channels
    share_rows = tap_rows // frame_devices
    padded_cols = -(-(col_count + 2) // 8) * 8
    right_pad = padded_cols - col_count - 1
    inverse_root = 1.0 / math.sqrt(total_frames * total_rows * col_count)
    weight_cube = weight.reshape(3, 3, 3, channels, channels)

    both_frames = lax.all_gather(
        jnp.concatenate([hidden, cotangent], axis=-1), "tm", axis=0, tiled=True
    )
    hidden_all = gather_rows(both_frames[..., :channels], height_count)
    framed = jnp.pad(hidden_all, ((2, 0), (1, 1), (1, right_pad), (0, 0)))

    cot_frames = both_frames[..., channels:]
    cot_all = lax.all_to_all(cot_frames, "height", split_axis=3, concat_axis=1, tiled=True)

    window = lax.dynamic_slice(
        framed,
        (frame_index * frame_count, row_index * row_count, 0, 0),
        (frame_count + 2, row_count + 2, padded_cols, channels),
    )
    conv_out = forward_conv(window, weight_cube, row_count, col_count).reshape(
        frame_count, row_count, col_count, channels
    )
    output = (latent_wide + conv_out + bias).astype(jnp.bfloat16)

    weight_grad = block_weight_grad(framed, cot_all, frame_index, share_rows, channels) * inverse_root

    cot_future = lax.dynamic_slice_in_dim(
        jnp.pad(cot_frames, ((0, 2), (0, 0), (0, 0), (0, 0))), frame_index * frame_count, 3, 0
    )
    cotangent_edged = padded(cot_future, (("height", 1),), 1)
    future_block = jnp.pad(cotangent_edged, ((0, 0), (0, 0), (1, right_pad), (0, 0)))
    hidden_grad = backward_conv(future_block, weight_cube, row_count, col_count).reshape(frame_count, row_count, col_count, channels)
    sigmoid_pre = jax.nn.sigmoid(normed)
    normed_grad = hidden_grad * sigmoid_pre * (1.0 + normed * (1.0 - sigmoid_pre))
    scaled_grad = normed_grad * gain
    unit_latent = latent_wide / root_mean
    inner = jnp.mean(scaled_grad * unit_latent, axis=-1, keepdims=True)
    latent_grad = (
        cotangent.astype(jnp.float32) + (scaled_grad - unit_latent * inner) / root_mean
    ).astype(jnp.bfloat16)
    return (output, latent_grad, weight_grad)


def solution(mesh):
    placed = (
        P(("grp", "tm"), "height", None, None),
        P(),
        P(),
        P(),
        P(("grp", "tm"), "height", None, None),
    )
    return jax.shard_map(
        local,
        mesh=mesh,
        in_specs=placed,
        out_specs=(
            P(("grp", "tm"), "height", None, None),
            P(("grp", "tm"), "height", None, None),
            P(("grp", "tm"), "height"),
        ),
        check_vma=False,
    )
```

```python
import math

import jax
import jax.numpy as jnp
from jax import lax
from jax.sharding import PartitionSpec as P


def shifted_2(value, axis, by):
    devices = lax.axis_size(axis)
    pairs = [(i, i + by) for i in range(devices) if 0 <= i + by < devices]
    return lax.ppermute(value, axis, pairs)


def padded(cells, sides, width):
    for axis, dim in sides:
        count = lax.axis_size(axis)
        ends = count - 1
        head = lax.slice_in_dim(cells, 0, width, axis=dim)
        tail = lax.slice_in_dim(cells, cells.shape[dim] - width, cells.shape[dim], axis=dim)
        cells = jnp.concatenate(
            [
                lax.ppermute(tail, axis, [(i, (i + 1) % count) for i in range(ends)]),
                cells,
                lax.ppermute(head, axis, [((i + 1) % count, i) for i in range(ends)]),
            ],
            axis=dim,
        )
    return cells


def forward_arrange(cube):
    depth, rows_t, cols_t, inputs, outputs = cube.shape
    return cube.transpose(0, 1, 3, 2, 4).reshape(9, inputs, 3 * outputs)


def backward_arrange(cube):
    depth, rows_t, cols_t, inputs, outputs = cube.shape
    return cube.transpose(0, 1, 4, 2, 3).reshape(9, outputs, 3 * inputs)


def forward_conv(window, cube, row_total, col_total):
    window = window[:, :, : col_total + 2]
    result = lax.conv_general_dilated(
        window[None],
        cube,
        (1, 1, 1),
        "VALID",
        dimension_numbers=("NDHWC", "DHWIO", "NDHWC"),
        preferred_element_type=jnp.float32,
    )
    return result[0, 0]


def backward_conv(window, cube, row_total, col_total):
    window = window[:, :, : col_total + 2]
    result = lax.conv_general_dilated(
        window[None],
        jnp.flip(cube, (0, 1, 2)),
        (1, 1, 1),
        "VALID",
        dimension_numbers=("NDHWC", "DHWOI", "NDHWC"),
        preferred_element_type=jnp.float32,
    )
    return result[0, 0]


def pair_count(tap_rows, share_rows, pair_rows, parts):
    most = 1
    for index in range(parts):
        first = index * share_rows
        last = first + share_rows - 1
        most = max(most, last // pair_rows - first // pair_rows + 1)
    return most


def depth_span(share_rows, tap_rows, channels):
    plane_rows = 9 * channels
    most = 1
    for index in range(tap_rows // share_rows):
        first = index * share_rows
        last = first + share_rows - 1
        most = max(most, last // plane_rows - first // plane_rows + 1)
    return most


def block_weight_grad(framed, cot_all, frame_index, share_rows, channels):
    frame_total, row_total, col_total, slots = cot_all.shape
    plane_rows = 9 * channels
    tap_rows = 27 * channels
    span = depth_span(share_rows, tap_rows, channels)
    first_row = frame_index * share_rows
    first_depth = jnp.minimum(first_row // plane_rows, 3 - span)
    frames = lax.dynamic_slice_in_dim(framed, first_depth, frame_total + span - 1, 0)
    frames = frames[:, :, : col_total + 2]
    terms = lax.conv_general_dilated(
        frames[..., None],
        cot_all[:, :, :, None, :],
        (1, 1, 1),
        "VALID",
        dimension_numbers=("DHWNC", "DHWIO", "DHWNC"),
        preferred_element_type=jnp.float32,
    ).reshape(span * plane_rows, slots)
    return lax.dynamic_slice_in_dim(terms, first_row - first_depth * plane_rows, share_rows, 0)


def gather_rows(own, height_count):
    frame_total, row_count, col_count, channels = own.shape
    height_index = lax.axis_index("height")
    core = height_index % 2
    chip = height_index // 2
    chips = height_count // 2
    first = core == 0
    sibling = [(i, i ^ 1) for i in range(height_count)]
    mine = [own] + [
        lax.ppermute(
            own, "height", [(i, (i + 2 * step) % height_count) for i in range(height_count)]
        )
        for step in range(1, chips)
    ]
    stacked = jnp.concatenate(mine, axis=1)
    twins = lax.ppermute(stacked, "height", sibling)
    block = 2 * row_count
    relative = []
    for step in reversed(range(chips)):
        ours = stacked[:, step * row_count : (step + 1) * row_count]
        theirs = twins[:, step * row_count : (step + 1) * row_count]
        relative.append(
            jnp.where(
                first,
                jnp.concatenate([ours, theirs], axis=1),
                jnp.concatenate([theirs, ours], axis=1),
            )
        )
    relative = jnp.concatenate(relative, axis=1)
    return jnp.concatenate(
        [
            lax.dynamic_slice_in_dim(relative, ((place - chip - 1) % chips) * block, block, 1)
            for place in range(chips)
        ],
        axis=1,
    )


def local(latents, gain, bias, weight, cotangent):
    frame_count, row_count, col_count, channels = latents.shape
    latent_wide = latents.astype(jnp.float32)
    root_mean = jnp.sqrt(jnp.mean(latent_wide * latent_wide, axis=-1, keepdims=True) + 1e-06)
    normed = latent_wide / root_mean * gain
    hidden = jax.nn.silu(normed).astype(jnp.bfloat16)
    height_count = lax.axis_size("height")
    frame_devices = lax.axis_size("tm")
    frame_index = lax.axis_index("tm")
    row_index = lax.axis_index("height")
    total_rows = row_count * height_count
    total_frames = frame_count * frame_devices
    tap_rows = 27 * channels
    share_rows = tap_rows // frame_devices
    padded_cols = col_count + 2
    right_pad = padded_cols - col_count - 1
    inverse_root = 1.0 / math.sqrt(total_frames * total_rows * col_count)
    weight_cube = weight.reshape(3, 3, 3, channels, channels)

    both_frames = lax.all_gather(
        jnp.concatenate([hidden, cotangent], axis=-1), "tm", axis=0, tiled=True
    )
    hidden_all = gather_rows(both_frames[..., :channels], height_count)
    framed = jnp.pad(hidden_all, ((2, 0), (1, 1), (1, right_pad), (0, 0)))

    cot_frames = both_frames[..., channels:]
    cot_all = lax.all_to_all(cot_frames, "height", split_axis=3, concat_axis=1, tiled=True)

    window = lax.dynamic_slice(
        framed,
        (frame_index * frame_count, row_index * row_count, 0, 0),
        (frame_count + 2, row_count + 2, padded_cols, channels),
    )
    conv_out = forward_conv(window, weight_cube, row_count, col_count).reshape(
        frame_count, row_count, col_count, channels
    )
    output = (latent_wide + conv_out + bias).astype(jnp.bfloat16)

    weight_grad = block_weight_grad(framed, cot_all, frame_index, share_rows, channels) * inverse_root

    cot_future = lax.dynamic_slice_in_dim(
        jnp.pad(cot_frames, ((0, 2), (0, 0), (0, 0), (0, 0))), frame_index * frame_count, 3, 0
    )
    cotangent_edged = padded(cot_future, (("height", 1),), 1)
    future_block = jnp.pad(cotangent_edged, ((0, 0), (0, 0), (1, right_pad), (0, 0)))
    hidden_grad = backward_conv(future_block, weight_cube, row_count, col_count).reshape(frame_count, row_count, col_count, channels)
    sigmoid_pre = jax.nn.sigmoid(normed)
    normed_grad = hidden_grad * sigmoid_pre * (1.0 + normed * (1.0 - sigmoid_pre))
    scaled_grad = normed_grad * gain
    unit_latent = latent_wide / root_mean
    inner = jnp.mean(scaled_grad * unit_latent, axis=-1, keepdims=True)
    latent_grad = (
        cotangent.astype(jnp.float32) + (scaled_grad - unit_latent * inner) / root_mean
    ).astype(jnp.bfloat16)
    return (output, latent_grad, weight_grad)


def solution(mesh):
    placed = (
        P(("grp", "tm"), "height", None, None),
        P(),
        P(),
        P(),
        P(("grp", "tm"), "height", None, None),
    )
    return jax.shard_map(
        local,
        mesh=mesh,
        in_specs=placed,
        out_specs=(
            P(("grp", "tm"), "height", None, None),
            P(("grp", "tm"), "height", None, None),
            P(("grp", "tm"), "height"),
        ),
        check_vma=False,
    )
```

```python
import math

import jax
import jax.numpy as jnp
from jax import lax
from jax.sharding import PartitionSpec as P


def shifted_2(value, axis, by):
    devices = lax.axis_size(axis)
    pairs = [(i, i + by) for i in range(devices) if 0 <= i + by < devices]
    return lax.ppermute(value, axis, pairs)


def padded(cells, sides, width):
    for axis, dim in sides:
        count = lax.axis_size(axis)
        ends = count - 1
        head = lax.slice_in_dim(cells, 0, width, axis=dim)
        tail = lax.slice_in_dim(cells, cells.shape[dim] - width, cells.shape[dim], axis=dim)
        cells = jnp.concatenate(
            [
                lax.ppermute(tail, axis, [(i, (i + 1) % count) for i in range(ends)]),
                cells,
                lax.ppermute(head, axis, [((i + 1) % count, i) for i in range(ends)]),
            ],
            axis=dim,
        )
    return cells


def forward_arrange(cube):
    depth, rows_t, cols_t, inputs, outputs = cube.shape
    return cube.transpose(0, 1, 3, 2, 4).reshape(9, inputs, 3 * outputs)


def backward_arrange(cube):
    depth, rows_t, cols_t, inputs, outputs = cube.shape
    return cube.transpose(0, 1, 4, 2, 3).reshape(9, outputs, 3 * inputs)


def forward_conv(window, cube, row_total, col_total):
    window = window[:, :, : col_total + 2]
    result = lax.conv_general_dilated(
        window[None],
        cube,
        (1, 1, 1),
        "VALID",
        dimension_numbers=("NDHWC", "DHWIO", "NDHWC"),
        preferred_element_type=jnp.float32,
    )
    return result[0, 0]


def backward_conv(window, cube, row_total, col_total):
    window = window[:, :, : col_total + 2]
    result = lax.conv_general_dilated(
        window[None],
        jnp.flip(cube, (0, 1, 2)),
        (1, 1, 1),
        "VALID",
        dimension_numbers=("NDHWC", "DHWOI", "NDHWC"),
        preferred_element_type=jnp.float32,
    )
    return result[0, 0]


def pair_count(tap_rows, share_rows, pair_rows, parts):
    most = 1
    for index in range(parts):
        first = index * share_rows
        last = first + share_rows - 1
        most = max(most, last // pair_rows - first // pair_rows + 1)
    return most


def block_weight_grad(framed, cot_all, frame_index, share_rows, channels):
    frame_total, row_total, col_total, slots = cot_all.shape
    padded_cols = framed.shape[2]
    pair_rows = 3 * channels
    tap_rows = 27 * channels
    flat_count = frame_total * row_total * padded_cols
    shifted = jnp.stack(
        [
            jnp.pad(
                cot_all,
                ((0, 0), (0, 0), (col_tap, padded_cols - col_total - col_tap), (0, 0)),
            )
            for col_tap in range(3)
        ],
        axis=3,
    )
    first_row = frame_index * share_rows
    first_pair = first_row // pair_rows
    count = pair_count(tap_rows, share_rows, pair_rows, tap_rows // share_rows)
    pieces = []
    for step in range(count):
        pair = jnp.minimum(first_pair + step, 8)
        depth_tap = pair // 3
        row_tap = pair % 3
        slab = lax.dynamic_slice(
            framed,
            (depth_tap, row_tap, 0, 0),
            (frame_total, row_total, padded_cols, channels),
        )
        product = lax.dot_general(
            shifted, slab, (((0, 1, 2), (0, 1, 2)), ((), ())), preferred_element_type=jnp.float32
        )
        pieces.append(product.transpose(0, 2, 1).reshape(pair_rows, slots))
    stacked = jnp.concatenate(pieces, axis=0)
    return lax.dynamic_slice_in_dim(stacked, first_row - first_pair * pair_rows, share_rows, 0)


def gather_rows(own, height_count):
    frame_total, row_count, col_count, channels = own.shape
    height_index = lax.axis_index("height")
    core = height_index % 2
    chip = height_index // 2
    chips = height_count // 2
    first = core == 0
    sibling = [(i, i ^ 1) for i in range(height_count)]
    mine = [own] + [
        lax.ppermute(
            own, "height", [(i, (i + 2 * step) % height_count) for i in range(height_count)]
        )
        for step in range(1, chips)
    ]
    stacked = jnp.concatenate(mine, axis=1)
    twins = lax.ppermute(stacked, "height", sibling)
    block = 2 * row_count
    relative = []
    for step in reversed(range(chips)):
        ours = stacked[:, step * row_count : (step + 1) * row_count]
        theirs = twins[:, step * row_count : (step + 1) * row_count]
        relative.append(
            jnp.where(
                first,
                jnp.concatenate([ours, theirs], axis=1),
                jnp.concatenate([theirs, ours], axis=1),
            )
        )
    relative = jnp.concatenate(relative, axis=1)
    return jnp.concatenate(
        [
            lax.dynamic_slice_in_dim(relative, ((place - chip - 1) % chips) * block, block, 1)
            for place in range(chips)
        ],
        axis=1,
    )


def local(latents, gain, bias, weight, cotangent):
    frame_count, row_count, col_count, channels = latents.shape
    latent_wide = latents.astype(jnp.float32)
    root_mean = jnp.sqrt(jnp.mean(latent_wide * latent_wide, axis=-1, keepdims=True) + 1e-06)
    normed = latent_wide / root_mean * gain
    hidden = jax.nn.silu(normed).astype(jnp.bfloat16)
    height_count = lax.axis_size("height")
    frame_devices = lax.axis_size("tm")
    frame_index = lax.axis_index("tm")
    row_index = lax.axis_index("height")
    total_rows = row_count * height_count
    total_frames = frame_count * frame_devices
    tap_rows = 27 * channels
    share_rows = tap_rows // frame_devices
    padded_cols = -(-(col_count + 2) // 8) * 8
    right_pad = padded_cols - col_count - 1
    inverse_root = 1.0 / math.sqrt(total_frames * total_rows * col_count)
    weight_cube = weight.reshape(3, 3, 3, channels, channels)

    both_frames = lax.all_gather(
        jnp.concatenate([hidden, cotangent], axis=-1), "tm", axis=0, tiled=True
    )
    hidden_all = gather_rows(both_frames[..., :channels], height_count)
    framed = jnp.pad(hidden_all, ((2, 0), (1, 1), (1, right_pad), (0, 0)))

    cot_frames = both_frames[..., channels:]
    cot_all = lax.all_to_all(cot_frames, "height", split_axis=3, concat_axis=1, tiled=True)

    window = lax.dynamic_slice(
        framed,
        (frame_index * frame_count, row_index * row_count, 0, 0),
        (frame_count + 2, row_count + 2, padded_cols, channels),
    )
    conv_out = forward_conv(window, weight_cube, row_count, col_count).reshape(
        frame_count, row_count, col_count, channels
    )
    output = (latent_wide + conv_out + bias).astype(jnp.bfloat16)

    weight_grad = block_weight_grad(framed, cot_all, frame_index, share_rows, channels) * inverse_root

    cot_future = lax.dynamic_slice_in_dim(
        jnp.pad(cot_frames, ((0, 2), (0, 0), (0, 0), (0, 0))), frame_index * frame_count, 3, 0
    )
    cotangent_edged = padded(cot_future, (("height", 1),), 1)
    future_block = jnp.pad(cotangent_edged, ((0, 0), (0, 0), (1, right_pad), (0, 0)))
    hidden_grad = backward_conv(future_block, weight_cube, row_count, col_count).reshape(frame_count, row_count, col_count, channels)
    sigmoid_pre = jax.nn.sigmoid(normed)
    normed_grad = hidden_grad * sigmoid_pre * (1.0 + normed * (1.0 - sigmoid_pre))
    scaled_grad = normed_grad * gain
    unit_latent = latent_wide / root_mean
    inner = jnp.mean(scaled_grad * unit_latent, axis=-1, keepdims=True)
    latent_grad = (
        cotangent.astype(jnp.float32) + (scaled_grad - unit_latent * inner) / root_mean
    ).astype(jnp.bfloat16)
    return (output, latent_grad, weight_grad)


def solution(mesh):
    placed = (
        P(("grp", "tm"), "height", None, None),
        P(),
        P(),
        P(),
        P(("grp", "tm"), "height", None, None),
    )
    return jax.shard_map(
        local,
        mesh=mesh,
        in_specs=placed,
        out_specs=(
            P(("grp", "tm"), "height", None, None),
            P(("grp", "tm"), "height", None, None),
            P(("grp", "tm"), "height"),
        ),
        check_vma=False,
    )
```

```python
import math

import jax
import jax.numpy as jnp
from jax import lax
from jax.sharding import PartitionSpec as P


def shifted_2(value, axis, by):
    devices = lax.axis_size(axis)
    pairs = [(i, i + by) for i in range(devices) if 0 <= i + by < devices]
    return lax.ppermute(value, axis, pairs)


def padded(cells, sides, width):
    for axis, dim in sides:
        count = lax.axis_size(axis)
        ends = count - 1
        head = lax.slice_in_dim(cells, 0, width, axis=dim)
        tail = lax.slice_in_dim(cells, cells.shape[dim] - width, cells.shape[dim], axis=dim)
        cells = jnp.concatenate(
            [
                lax.ppermute(tail, axis, [(i, (i + 1) % count) for i in range(ends)]),
                cells,
                lax.ppermute(head, axis, [((i + 1) % count, i) for i in range(ends)]),
            ],
            axis=dim,
        )
    return cells


def forward_arrange(cube):
    depth, rows_t, cols_t, inputs, outputs = cube.shape
    return cube.transpose(0, 1, 3, 2, 4).reshape(9, inputs, 3 * outputs)


def backward_arrange(cube):
    depth, rows_t, cols_t, inputs, outputs = cube.shape
    return cube.transpose(0, 1, 4, 2, 3).reshape(9, outputs, 3 * inputs)


def forward_conv(window, cube, row_total, col_total):
    window = window[:, :, : col_total + 2]
    result = lax.conv_general_dilated(
        window[None],
        cube,
        (1, 1, 1),
        "VALID",
        dimension_numbers=("NDHWC", "DHWIO", "NDHWC"),
        preferred_element_type=jnp.float32,
    )
    return result[0, 0]


def backward_conv(window, cube, row_total, col_total):
    window = window[:, :, : col_total + 2]
    result = lax.conv_general_dilated(
        window[None],
        jnp.flip(cube, (0, 1, 2)),
        (1, 1, 1),
        "VALID",
        dimension_numbers=("NDHWC", "DHWOI", "NDHWC"),
        preferred_element_type=jnp.float32,
    )
    return result[0, 0]


def pair_count(tap_rows, share_rows, pair_rows, parts):
    most = 1
    for index in range(parts):
        first = index * share_rows
        last = first + share_rows - 1
        most = max(most, last // pair_rows - first // pair_rows + 1)
    return most


def block_weight_grad(framed, cot_all, frame_index, share_rows, channels):
    frame_total, row_total, col_total, slots = cot_all.shape
    padded_cols = framed.shape[2]
    pair_rows = 3 * channels
    tap_rows = 27 * channels
    flat_count = frame_total * row_total * padded_cols
    shifted = jnp.stack(
        [
            jnp.pad(
                cot_all,
                ((0, 0), (0, 0), (col_tap, padded_cols - col_total - col_tap), (0, 0)),
            )
            for col_tap in range(3)
        ],
        axis=3,
    )
    first_row = frame_index * share_rows
    first_pair = first_row // pair_rows
    count = pair_count(tap_rows, share_rows, pair_rows, tap_rows // share_rows)
    pieces = []
    for step in range(count):
        pair = jnp.minimum(first_pair + step, 8)
        depth_tap = pair // 3
        row_tap = pair % 3
        slab = lax.dynamic_slice(
            framed,
            (depth_tap, row_tap, 0, 0),
            (frame_total, row_total, padded_cols, channels),
        )
        product = lax.dot_general(
            shifted, slab, (((0, 1, 2), (0, 1, 2)), ((), ())), preferred_element_type=jnp.float32
        )
        pieces.append(product.transpose(0, 2, 1).reshape(pair_rows, slots))
    stacked = jnp.concatenate(pieces, axis=0)
    return lax.dynamic_slice_in_dim(stacked, first_row - first_pair * pair_rows, share_rows, 0)


def gather_rows(own, height_count):
    frame_total, row_count, col_count, channels = own.shape
    height_index = lax.axis_index("height")
    core = height_index % 2
    chip = height_index // 2
    chips = height_count // 2
    first = core == 0
    sibling = [(i, i ^ 1) for i in range(height_count)]
    mine = [own] + [
        lax.ppermute(
            own, "height", [(i, (i + 2 * step) % height_count) for i in range(height_count)]
        )
        for step in range(1, chips)
    ]
    stacked = jnp.concatenate(mine, axis=1)
    twins = lax.ppermute(stacked, "height", sibling)
    block = 2 * row_count
    relative = []
    for step in reversed(range(chips)):
        ours = stacked[:, step * row_count : (step + 1) * row_count]
        theirs = twins[:, step * row_count : (step + 1) * row_count]
        relative.append(
            jnp.where(
                first,
                jnp.concatenate([ours, theirs], axis=1),
                jnp.concatenate([theirs, ours], axis=1),
            )
        )
    relative = jnp.concatenate(relative, axis=1)
    return jnp.concatenate(
        [
            lax.dynamic_slice_in_dim(relative, ((place - chip - 1) % chips) * block, block, 1)
            for place in range(chips)
        ],
        axis=1,
    )


def gather_frames(block):
    count = lax.axis_size("tm")
    position = lax.axis_index("tm")
    up = [(i, i + 1) for i in range(count - 1)]
    down = [(i + 1, i) for i in range(count - 1)]
    earlier, later = [], []
    rising, falling = block, block
    for step in range(1, count):
        rising = lax.ppermute(rising, "tm", up)
        falling = lax.ppermute(falling, "tm", down)
        earlier.append(rising)
        later.append(falling)
    relative = jnp.concatenate(earlier[::-1] + [block] + later, axis=0)
    return lax.dynamic_slice_in_dim(relative, count - 1 - position, count * block.shape[0], 0)


def local(latents, gain, bias, weight, cotangent):
    frame_count, row_count, col_count, channels = latents.shape
    latent_wide = latents.astype(jnp.float32)
    root_mean = jnp.sqrt(jnp.mean(latent_wide * latent_wide, axis=-1, keepdims=True) + 1e-06)
    normed = latent_wide / root_mean * gain
    hidden = jax.nn.silu(normed).astype(jnp.bfloat16)
    height_count = lax.axis_size("height")
    frame_devices = lax.axis_size("tm")
    frame_index = lax.axis_index("tm")
    row_index = lax.axis_index("height")
    total_rows = row_count * height_count
    total_frames = frame_count * frame_devices
    tap_rows = 27 * channels
    share_rows = tap_rows // frame_devices
    padded_cols = -(-(col_count + 2) // 8) * 8
    right_pad = padded_cols - col_count - 1
    inverse_root = 1.0 / math.sqrt(total_frames * total_rows * col_count)
    weight_cube = weight.reshape(3, 3, 3, channels, channels)

    both_frames = gather_frames(jnp.concatenate([hidden, cotangent], axis=-1))
    hidden_all = gather_rows(both_frames[..., :channels], height_count)
    framed = jnp.pad(hidden_all, ((2, 0), (1, 1), (1, right_pad), (0, 0)))

    cot_frames = both_frames[..., channels:]
    cot_all = lax.all_to_all(cot_frames, "height", split_axis=3, concat_axis=1, tiled=True)

    window = lax.dynamic_slice(
        framed,
        (frame_index * frame_count, row_index * row_count, 0, 0),
        (frame_count + 2, row_count + 2, padded_cols, channels),
    )
    conv_out = forward_conv(window, weight_cube, row_count, col_count).reshape(
        frame_count, row_count, col_count, channels
    )
    output = (latent_wide + conv_out + bias).astype(jnp.bfloat16)

    weight_grad = block_weight_grad(framed, cot_all, frame_index, share_rows, channels) * inverse_root

    cot_future = lax.dynamic_slice_in_dim(
        jnp.pad(cot_frames, ((0, 2), (0, 0), (0, 0), (0, 0))), frame_index * frame_count, 3, 0
    )
    cotangent_edged = padded(cot_future, (("height", 1),), 1)
    future_block = jnp.pad(cotangent_edged, ((0, 0), (0, 0), (1, right_pad), (0, 0)))
    hidden_grad = backward_conv(future_block, weight_cube, row_count, col_count).reshape(frame_count, row_count, col_count, channels)
    sigmoid_pre = jax.nn.sigmoid(normed)
    normed_grad = hidden_grad * sigmoid_pre * (1.0 + normed * (1.0 - sigmoid_pre))
    scaled_grad = normed_grad * gain
    unit_latent = latent_wide / root_mean
    inner = jnp.mean(scaled_grad * unit_latent, axis=-1, keepdims=True)
    latent_grad = (
        cotangent.astype(jnp.float32) + (scaled_grad - unit_latent * inner) / root_mean
    ).astype(jnp.bfloat16)
    return (output, latent_grad, weight_grad)


def solution(mesh):
    placed = (
        P(("grp", "tm"), "height", None, None),
        P(),
        P(),
        P(),
        P(("grp", "tm"), "height", None, None),
    )
    return jax.shard_map(
        local,
        mesh=mesh,
        in_specs=placed,
        out_specs=(
            P(("grp", "tm"), "height", None, None),
            P(("grp", "tm"), "height", None, None),
            P(("grp", "tm"), "height"),
        ),
        check_vma=False,
    )
```

```python
import math

import jax
import jax.numpy as jnp
from jax import lax
from jax.sharding import PartitionSpec as P


def shifted_2(value, axis, by):
    devices = lax.axis_size(axis)
    pairs = [(i, i + by) for i in range(devices) if 0 <= i + by < devices]
    return lax.ppermute(value, axis, pairs)


def padded(cells, sides, width):
    for axis, dim in sides:
        count = lax.axis_size(axis)
        ends = count - 1
        head = lax.slice_in_dim(cells, 0, width, axis=dim)
        tail = lax.slice_in_dim(cells, cells.shape[dim] - width, cells.shape[dim], axis=dim)
        cells = jnp.concatenate(
            [
                lax.ppermute(tail, axis, [(i, (i + 1) % count) for i in range(ends)]),
                cells,
                lax.ppermute(head, axis, [((i + 1) % count, i) for i in range(ends)]),
            ],
            axis=dim,
        )
    return cells


def forward_arrange(cube):
    depth, rows_t, cols_t, inputs, outputs = cube.shape
    return cube.transpose(0, 1, 3, 2, 4).reshape(9, inputs, 3 * outputs)


def backward_arrange(cube):
    depth, rows_t, cols_t, inputs, outputs = cube.shape
    return cube.transpose(0, 1, 4, 2, 3).reshape(9, outputs, 3 * inputs)


def forward_conv(window, cube, row_total, col_total):
    window = window[:, :, : col_total + 2]
    result = lax.conv_general_dilated(
        window[None],
        cube,
        (1, 1, 1),
        "VALID",
        dimension_numbers=("NDHWC", "DHWIO", "NDHWC"),
        preferred_element_type=jnp.float32,
    )
    return result[0, 0]


def backward_conv(window, cube, row_total, col_total):
    window = window[:, :, : col_total + 2]
    result = lax.conv_general_dilated(
        window[None],
        jnp.flip(cube, (0, 1, 2)),
        (1, 1, 1),
        "VALID",
        dimension_numbers=("NDHWC", "DHWOI", "NDHWC"),
        preferred_element_type=jnp.float32,
    )
    return result[0, 0]


def pair_count(tap_rows, share_rows, pair_rows, parts):
    most = 1
    for index in range(parts):
        first = index * share_rows
        last = first + share_rows - 1
        most = max(most, last // pair_rows - first // pair_rows + 1)
    return most


def block_weight_grad(framed, cot_all, frame_index, share_rows, channels):
    frame_total, row_total, col_total, slots = cot_all.shape
    padded_cols = framed.shape[2]
    pair_rows = 3 * channels
    tap_rows = 27 * channels
    flat_count = frame_total * row_total * padded_cols
    shifted = jnp.stack(
        [
            jnp.pad(
                cot_all,
                ((0, 0), (0, 0), (col_tap, padded_cols - col_total - col_tap), (0, 0)),
            )
            for col_tap in range(3)
        ],
        axis=3,
    )
    first_row = frame_index * share_rows
    first_pair = first_row // pair_rows
    count = pair_count(tap_rows, share_rows, pair_rows, tap_rows // share_rows)
    pieces = []
    for step in range(count):
        pair = jnp.minimum(first_pair + step, 8)
        depth_tap = pair // 3
        row_tap = pair % 3
        slab = lax.dynamic_slice(
            framed,
            (depth_tap, row_tap, 0, 0),
            (frame_total, row_total, padded_cols, channels),
        )
        product = lax.dot_general(
            shifted, slab, (((0, 1, 2), (0, 1, 2)), ((), ())), preferred_element_type=jnp.float32
        )
        pieces.append(product.transpose(0, 2, 1).reshape(pair_rows, slots))
    stacked = jnp.concatenate(pieces, axis=0)
    return lax.dynamic_slice_in_dim(stacked, first_row - first_pair * pair_rows, share_rows, 0)


def gather_rows(own, height_count):
    frame_total, row_count, col_count, channels = own.shape
    height_index = lax.axis_index("height")
    core = height_index % 2
    chip = height_index // 2
    chips = height_count // 2
    first = core == 0
    sibling = [(i, i ^ 1) for i in range(height_count)]
    mine = [own] + [
        lax.ppermute(
            own, "height", [(i, (i + 2 * step) % height_count) for i in range(height_count)]
        )
        for step in range(1, chips)
    ]
    stacked = jnp.concatenate(mine, axis=1)
    twins = lax.ppermute(stacked, "height", sibling)
    block = 2 * row_count
    relative = []
    for step in reversed(range(chips)):
        ours = stacked[:, step * row_count : (step + 1) * row_count]
        theirs = twins[:, step * row_count : (step + 1) * row_count]
        relative.append(
            jnp.where(
                first,
                jnp.concatenate([ours, theirs], axis=1),
                jnp.concatenate([theirs, ours], axis=1),
            )
        )
    relative = jnp.concatenate(relative, axis=1)
    return jnp.concatenate(
        [
            lax.dynamic_slice_in_dim(relative, ((place - chip - 1) % chips) * block, block, 1)
            for place in range(chips)
        ],
        axis=1,
    )


def gather_frames(block):
    count = lax.axis_size("tm")
    up = [(i, i + 1) for i in range(count - 1)]
    down = [(i + 1, i) for i in range(count - 1)]
    groups = [block]
    rising, falling = block, block
    for step in range(1, count):
        rising = lax.ppermute(rising, "tm", up)
        falling = lax.ppermute(falling, "tm", down)
        groups.append(jnp.concatenate([rising, falling], axis=0))
    return groups


def in_order(groups):
    count = len(groups)
    position = lax.axis_index("tm")
    size = groups[0].shape[0]
    relative = jnp.concatenate(
        [groups[step][:size] for step in reversed(range(1, count))]
        + [groups[0]]
        + [groups[step][size:] for step in range(1, count)],
        axis=0,
    )
    return lax.dynamic_slice_in_dim(relative, (count - 1 - position) * size, count * size, 0)


def place_frames(groups, offsets, frame_total, padded_cols):
    position = lax.axis_index("tm")
    _, row_total, _, channels = groups[0].shape
    framed = jnp.zeros(
        (frame_total + 2, row_total + 2, padded_cols, channels), groups[0].dtype
    )
    writes = [
        (abs(offset), group[index : index + 1], offset)
        for group, shifts in zip(groups, offsets)
        for index, offset in enumerate(shifts)
    ]
    for _, piece, offset in sorted(writes, key=lambda item: -item[0]):
        framed = lax.dynamic_update_slice(framed, piece, (2 + position + offset, 1, 1, 0))
    return framed


def local(latents, gain, bias, weight, cotangent):
    frame_count, row_count, col_count, channels = latents.shape
    latent_wide = latents.astype(jnp.float32)
    root_mean = jnp.sqrt(jnp.mean(latent_wide * latent_wide, axis=-1, keepdims=True) + 1e-06)
    normed = latent_wide / root_mean * gain
    hidden = jax.nn.silu(normed).astype(jnp.bfloat16)
    height_count = lax.axis_size("height")
    frame_devices = lax.axis_size("tm")
    frame_index = lax.axis_index("tm")
    row_index = lax.axis_index("height")
    total_rows = row_count * height_count
    total_frames = frame_count * frame_devices
    tap_rows = 27 * channels
    share_rows = tap_rows // frame_devices
    padded_cols = -(-(col_count + 2) // 8) * 8
    right_pad = padded_cols - col_count - 1
    inverse_root = 1.0 / math.sqrt(total_frames * total_rows * col_count)
    weight_cube = weight.reshape(3, 3, 3, channels, channels)

    groups = gather_frames(jnp.concatenate([hidden, cotangent], axis=-1))
    both_frames = in_order(groups)
    if len(groups) <= 4:
        framed = place_frames(
            [gather_rows(group[..., :channels], height_count) for group in groups],
            [[0]] + [[-step, step] for step in range(1, len(groups))],
            total_frames,
            padded_cols,
        )
    else:
        hidden_all = gather_rows(both_frames[..., :channels], height_count)
        framed = jnp.pad(hidden_all, ((2, 0), (1, 1), (1, right_pad), (0, 0)))

    cot_frames = both_frames[..., channels:]
    cot_all = lax.all_to_all(cot_frames, "height", split_axis=3, concat_axis=1, tiled=True)

    window = lax.dynamic_slice(
        framed,
        (frame_index * frame_count, row_index * row_count, 0, 0),
        (frame_count + 2, row_count + 2, padded_cols, channels),
    )
    conv_out = forward_conv(window, weight_cube, row_count, col_count).reshape(
        frame_count, row_count, col_count, channels
    )
    output = (latent_wide + conv_out + bias).astype(jnp.bfloat16)

    weight_grad = block_weight_grad(framed, cot_all, frame_index, share_rows, channels) * inverse_root

    cot_future = lax.dynamic_slice_in_dim(
        jnp.pad(cot_frames, ((0, 2), (0, 0), (0, 0), (0, 0))), frame_index * frame_count, 3, 0
    )
    cotangent_edged = padded(cot_future, (("height", 1),), 1)
    future_block = jnp.pad(cotangent_edged, ((0, 0), (0, 0), (1, right_pad), (0, 0)))
    hidden_grad = backward_conv(future_block, weight_cube, row_count, col_count).reshape(frame_count, row_count, col_count, channels)
    sigmoid_pre = jax.nn.sigmoid(normed)
    normed_grad = hidden_grad * sigmoid_pre * (1.0 + normed * (1.0 - sigmoid_pre))
    scaled_grad = normed_grad * gain
    unit_latent = latent_wide / root_mean
    inner = jnp.mean(scaled_grad * unit_latent, axis=-1, keepdims=True)
    latent_grad = (
        cotangent.astype(jnp.float32) + (scaled_grad - unit_latent * inner) / root_mean
    ).astype(jnp.bfloat16)
    return (output, latent_grad, weight_grad)


def solution(mesh):
    placed = (
        P(("grp", "tm"), "height", None, None),
        P(),
        P(),
        P(),
        P(("grp", "tm"), "height", None, None),
    )
    return jax.shard_map(
        local,
        mesh=mesh,
        in_specs=placed,
        out_specs=(
            P(("grp", "tm"), "height", None, None),
            P(("grp", "tm"), "height", None, None),
            P(("grp", "tm"), "height"),
        ),
        check_vma=False,
    )
```

```python
import math

import jax
import jax.numpy as jnp
from jax import lax
from jax.sharding import PartitionSpec as P


def shifted_2(value, axis, by):
    devices = lax.axis_size(axis)
    pairs = [(i, i + by) for i in range(devices) if 0 <= i + by < devices]
    return lax.ppermute(value, axis, pairs)


def padded(cells, sides, width):
    for axis, dim in sides:
        count = lax.axis_size(axis)
        ends = count - 1
        head = lax.slice_in_dim(cells, 0, width, axis=dim)
        tail = lax.slice_in_dim(cells, cells.shape[dim] - width, cells.shape[dim], axis=dim)
        cells = jnp.concatenate(
            [
                lax.ppermute(tail, axis, [(i, (i + 1) % count) for i in range(ends)]),
                cells,
                lax.ppermute(head, axis, [((i + 1) % count, i) for i in range(ends)]),
            ],
            axis=dim,
        )
    return cells


def forward_arrange(cube):
    depth, rows_t, cols_t, inputs, outputs = cube.shape
    return cube.transpose(0, 1, 3, 2, 4).reshape(9, inputs, 3 * outputs)


def backward_arrange(cube):
    depth, rows_t, cols_t, inputs, outputs = cube.shape
    return cube.transpose(0, 1, 4, 2, 3).reshape(9, outputs, 3 * inputs)


def forward_conv(window, cube, row_total, col_total):
    window = window[:, :, : col_total + 2]
    result = lax.conv_general_dilated(
        window[None],
        cube,
        (1, 1, 1),
        "VALID",
        dimension_numbers=("NDHWC", "DHWIO", "NDHWC"),
        preferred_element_type=jnp.float32,
    )
    return result[0, 0]


def backward_conv(window, cube, row_total, col_total):
    window = window[:, :, : col_total + 2]
    result = lax.conv_general_dilated(
        window[None],
        jnp.flip(cube, (0, 1, 2)),
        (1, 1, 1),
        "VALID",
        dimension_numbers=("NDHWC", "DHWOI", "NDHWC"),
        preferred_element_type=jnp.float32,
    )
    return result[0, 0]


def pair_count(tap_rows, share_rows, pair_rows, parts):
    most = 1
    for index in range(parts):
        first = index * share_rows
        last = first + share_rows - 1
        most = max(most, last // pair_rows - first // pair_rows + 1)
    return most


def block_weight_grad(framed, cot_all, frame_index, share_rows, channels):
    frame_total, row_total, col_total, slots = cot_all.shape
    padded_cols = framed.shape[2]
    pair_rows = 3 * channels
    tap_rows = 27 * channels
    flat_count = frame_total * row_total * padded_cols
    shifted = jnp.stack(
        [
            jnp.pad(
                cot_all,
                ((0, 0), (0, 0), (col_tap, padded_cols - col_total - col_tap), (0, 0)),
            )
            for col_tap in range(3)
        ],
        axis=3,
    )
    first_row = frame_index * share_rows
    first_pair = first_row // pair_rows
    count = pair_count(tap_rows, share_rows, pair_rows, tap_rows // share_rows)
    pieces = []
    for step in range(count):
        pair = jnp.minimum(first_pair + step, 8)
        depth_tap = pair // 3
        row_tap = pair % 3
        slab = lax.dynamic_slice(
            framed,
            (depth_tap, row_tap, 0, 0),
            (frame_total, row_total, padded_cols, channels),
        )
        product = lax.dot_general(
            shifted, slab, (((0, 1, 2), (0, 1, 2)), ((), ())), preferred_element_type=jnp.float32
        )
        pieces.append(product.transpose(0, 2, 1).reshape(pair_rows, slots))
    stacked = jnp.concatenate(pieces, axis=0)
    return lax.dynamic_slice_in_dim(stacked, first_row - first_pair * pair_rows, share_rows, 0)


def gather_rows(own, height_count):
    frame_total, row_count, col_count, channels = own.shape
    height_index = lax.axis_index("height")
    core = height_index % 2
    chip = height_index // 2
    chips = height_count // 2
    first = core == 0
    sibling = [(i, i ^ 1) for i in range(height_count)]
    mine = [own] + [
        lax.ppermute(
            own, "height", [(i, (i + 2 * step) % height_count) for i in range(height_count)]
        )
        for step in range(1, chips)
    ]
    stacked = jnp.concatenate(mine, axis=1)
    twins = lax.ppermute(stacked, "height", sibling)
    block = 2 * row_count
    relative = []
    for step in reversed(range(chips)):
        ours = stacked[:, step * row_count : (step + 1) * row_count]
        theirs = twins[:, step * row_count : (step + 1) * row_count]
        relative.append(
            jnp.where(
                first,
                jnp.concatenate([ours, theirs], axis=1),
                jnp.concatenate([theirs, ours], axis=1),
            )
        )
    relative = jnp.concatenate(relative, axis=1)
    return jnp.concatenate(
        [
            lax.dynamic_slice_in_dim(relative, ((place - chip - 1) % chips) * block, block, 1)
            for place in range(chips)
        ],
        axis=1,
    )


def gather_frames(block):
    count = lax.axis_size("tm")
    position = lax.axis_index("tm")
    earlier = [
        lax.ppermute(block, "tm", [(i, i + step) for i in range(count - step)])
        for step in range(1, count)
    ]
    later = [
        lax.ppermute(block, "tm", [(i + step, i) for i in range(count - step)])
        for step in range(1, count)
    ]
    relative = jnp.concatenate(earlier[::-1] + [block] + later, axis=0)
    return lax.dynamic_slice_in_dim(relative, count - 1 - position, count * block.shape[0], 0)


def local(latents, gain, bias, weight, cotangent):
    frame_count, row_count, col_count, channels = latents.shape
    latent_wide = latents.astype(jnp.float32)
    root_mean = jnp.sqrt(jnp.mean(latent_wide * latent_wide, axis=-1, keepdims=True) + 1e-06)
    normed = latent_wide / root_mean * gain
    hidden = jax.nn.silu(normed).astype(jnp.bfloat16)
    height_count = lax.axis_size("height")
    frame_devices = lax.axis_size("tm")
    frame_index = lax.axis_index("tm")
    row_index = lax.axis_index("height")
    total_rows = row_count * height_count
    total_frames = frame_count * frame_devices
    tap_rows = 27 * channels
    share_rows = tap_rows // frame_devices
    padded_cols = -(-(col_count + 2) // 8) * 8
    right_pad = padded_cols - col_count - 1
    inverse_root = 1.0 / math.sqrt(total_frames * total_rows * col_count)
    weight_cube = weight.reshape(3, 3, 3, channels, channels)

    both_frames = gather_frames(jnp.concatenate([hidden, cotangent], axis=-1))
    hidden_all = gather_rows(both_frames[..., :channels], height_count)
    framed = jnp.pad(hidden_all, ((2, 0), (1, 1), (1, right_pad), (0, 0)))

    cot_frames = both_frames[..., channels:]
    cot_all = lax.all_to_all(cot_frames, "height", split_axis=3, concat_axis=1, tiled=True)

    window = lax.dynamic_slice(
        framed,
        (frame_index * frame_count, row_index * row_count, 0, 0),
        (frame_count + 2, row_count + 2, padded_cols, channels),
    )
    conv_out = forward_conv(window, weight_cube, row_count, col_count).reshape(
        frame_count, row_count, col_count, channels
    )
    output = (latent_wide + conv_out + bias).astype(jnp.bfloat16)

    weight_grad = block_weight_grad(framed, cot_all, frame_index, share_rows, channels) * inverse_root

    cot_future = lax.dynamic_slice_in_dim(
        jnp.pad(cot_frames, ((0, 2), (0, 0), (0, 0), (0, 0))), frame_index * frame_count, 3, 0
    )
    cotangent_edged = padded(cot_future, (("height", 1),), 1)
    future_block = jnp.pad(cotangent_edged, ((0, 0), (0, 0), (1, right_pad), (0, 0)))
    hidden_grad = backward_conv(future_block, weight_cube, row_count, col_count).reshape(frame_count, row_count, col_count, channels)
    sigmoid_pre = jax.nn.sigmoid(normed)
    normed_grad = hidden_grad * sigmoid_pre * (1.0 + normed * (1.0 - sigmoid_pre))
    scaled_grad = normed_grad * gain
    unit_latent = latent_wide / root_mean
    inner = jnp.mean(scaled_grad * unit_latent, axis=-1, keepdims=True)
    latent_grad = (
        cotangent.astype(jnp.float32) + (scaled_grad - unit_latent * inner) / root_mean
    ).astype(jnp.bfloat16)
    return (output, latent_grad, weight_grad)


def solution(mesh):
    placed = (
        P(("grp", "tm"), "height", None, None),
        P(),
        P(),
        P(),
        P(("grp", "tm"), "height", None, None),
    )
    return jax.shard_map(
        local,
        mesh=mesh,
        in_specs=placed,
        out_specs=(
            P(("grp", "tm"), "height", None, None),
            P(("grp", "tm"), "height", None, None),
            P(("grp", "tm"), "height"),
        ),
        check_vma=False,
    )
```

```python
import math

import jax
import jax.numpy as jnp
from jax import lax
from jax.sharding import PartitionSpec as P


def shifted_2(value, axis, by):
    devices = lax.axis_size(axis)
    pairs = [(i, i + by) for i in range(devices) if 0 <= i + by < devices]
    return lax.ppermute(value, axis, pairs)


def padded(cells, sides, width):
    for axis, dim in sides:
        count = lax.axis_size(axis)
        ends = count - 1
        head = lax.slice_in_dim(cells, 0, width, axis=dim)
        tail = lax.slice_in_dim(cells, cells.shape[dim] - width, cells.shape[dim], axis=dim)
        cells = jnp.concatenate(
            [
                lax.ppermute(tail, axis, [(i, (i + 1) % count) for i in range(ends)]),
                cells,
                lax.ppermute(head, axis, [((i + 1) % count, i) for i in range(ends)]),
            ],
            axis=dim,
        )
    return cells


def forward_arrange(cube):
    depth, rows_t, cols_t, inputs, outputs = cube.shape
    return cube.transpose(0, 1, 3, 2, 4).reshape(9, inputs, 3 * outputs)


def backward_arrange(cube):
    depth, rows_t, cols_t, inputs, outputs = cube.shape
    return cube.transpose(0, 1, 4, 2, 3).reshape(9, outputs, 3 * inputs)


def forward_conv(window, cube, row_total, col_total):
    window = window[:, :, : col_total + 2]
    result = lax.conv_general_dilated(
        window[None],
        cube,
        (1, 1, 1),
        "VALID",
        dimension_numbers=("NDHWC", "DHWIO", "NDHWC"),
        preferred_element_type=jnp.float32,
    )
    return result[0, 0]


def backward_conv(window, cube, row_total, col_total):
    window = window[:, :, : col_total + 2]
    result = lax.conv_general_dilated(
        window[None],
        jnp.flip(cube, (0, 1, 2)),
        (1, 1, 1),
        "VALID",
        dimension_numbers=("NDHWC", "DHWOI", "NDHWC"),
        preferred_element_type=jnp.float32,
    )
    return result[0, 0]


def pair_count(tap_rows, share_rows, pair_rows, parts):
    most = 1
    for index in range(parts):
        first = index * share_rows
        last = first + share_rows - 1
        most = max(most, last // pair_rows - first // pair_rows + 1)
    return most


def block_weight_grad(framed, cot_all, frame_index, share_rows, channels):
    frame_total, row_total, col_total, slots = cot_all.shape
    padded_cols = framed.shape[2]
    pair_rows = 3 * channels
    tap_rows = 27 * channels
    flat_count = frame_total * row_total * padded_cols
    shifted = jnp.stack(
        [
            jnp.pad(
                cot_all,
                ((0, 0), (0, 0), (col_tap, padded_cols - col_total - col_tap), (0, 0)),
            )
            for col_tap in range(3)
        ],
        axis=3,
    )
    first_row = frame_index * share_rows
    first_pair = first_row // pair_rows
    count = pair_count(tap_rows, share_rows, pair_rows, tap_rows // share_rows)
    pieces = []
    for step in range(count):
        pair = jnp.minimum(first_pair + step, 8)
        depth_tap = pair // 3
        row_tap = pair % 3
        slab = lax.dynamic_slice(
            framed,
            (depth_tap, row_tap, 0, 0),
            (frame_total, row_total, padded_cols, channels),
        )
        product = lax.dot_general(
            shifted, slab, (((0, 1, 2), (0, 1, 2)), ((), ())), preferred_element_type=jnp.float32
        )
        pieces.append(product.transpose(0, 2, 1).reshape(pair_rows, slots))
    stacked = jnp.concatenate(pieces, axis=0)
    return lax.dynamic_slice_in_dim(stacked, first_row - first_pair * pair_rows, share_rows, 0)


def gather_rows(own, height_count):
    frame_total, row_count, col_count, channels = own.shape
    height_index = lax.axis_index("height")
    core = height_index % 2
    chip = height_index // 2
    chips = height_count // 2
    first = core == 0
    sibling = [(i, i ^ 1) for i in range(height_count)]
    mine = [own] + [
        lax.ppermute(
            own, "height", [(i, (i + 2 * step) % height_count) for i in range(height_count)]
        )
        for step in range(1, chips)
    ]
    stacked = jnp.concatenate(mine, axis=1)
    twins = lax.ppermute(stacked, "height", sibling)
    block = 2 * row_count
    relative = []
    for step in reversed(range(chips)):
        ours = stacked[:, step * row_count : (step + 1) * row_count]
        theirs = twins[:, step * row_count : (step + 1) * row_count]
        relative.append(
            jnp.where(
                first,
                jnp.concatenate([ours, theirs], axis=1),
                jnp.concatenate([theirs, ours], axis=1),
            )
        )
    relative = jnp.concatenate(relative, axis=1)
    return jnp.concatenate(
        [
            lax.dynamic_slice_in_dim(relative, ((place - chip - 1) % chips) * block, block, 1)
            for place in range(chips)
        ],
        axis=1,
    )


def gather_frames(block):
    count = lax.axis_size("tm")
    up = [(i, i + 1) for i in range(count - 1)]
    down = [(i + 1, i) for i in range(count - 1)]
    groups = [block]
    rising, falling = block, block
    for step in range(1, count):
        rising = lax.ppermute(rising, "tm", up)
        falling = lax.ppermute(falling, "tm", down)
        groups.append(jnp.concatenate([rising, falling], axis=0))
    return groups


def in_order(groups):
    count = len(groups)
    position = lax.axis_index("tm")
    size = groups[0].shape[0]
    relative = jnp.concatenate(
        [groups[step][:size] for step in reversed(range(1, count))]
        + [groups[0]]
        + [groups[step][size:] for step in range(1, count)],
        axis=0,
    )
    return lax.dynamic_slice_in_dim(relative, (count - 1 - position) * size, count * size, 0)


def local(latents, gain, bias, weight, cotangent):
    frame_count, row_count, col_count, channels = latents.shape
    latent_wide = latents.astype(jnp.float32)
    root_mean = jnp.sqrt(jnp.mean(latent_wide * latent_wide, axis=-1, keepdims=True) + 1e-06)
    normed = latent_wide / root_mean * gain
    hidden = jax.nn.silu(normed).astype(jnp.bfloat16)
    height_count = lax.axis_size("height")
    frame_devices = lax.axis_size("tm")
    frame_index = lax.axis_index("tm")
    row_index = lax.axis_index("height")
    total_rows = row_count * height_count
    total_frames = frame_count * frame_devices
    tap_rows = 27 * channels
    share_rows = tap_rows // frame_devices
    padded_cols = -(-(col_count + 2) // 8) * 8
    right_pad = padded_cols - col_count - 1
    inverse_root = 1.0 / math.sqrt(total_frames * total_rows * col_count)
    weight_cube = weight.reshape(3, 3, 3, channels, channels)

    groups = gather_frames(jnp.concatenate([hidden, cotangent], axis=-1))
    both_frames = in_order(groups)
    if len(groups) <= 4:
        hidden_all = in_order([gather_rows(group[..., :channels], height_count) for group in groups])
    else:
        hidden_all = gather_rows(both_frames[..., :channels], height_count)
    framed = jnp.pad(hidden_all, ((2, 0), (1, 1), (1, right_pad), (0, 0)))

    cot_frames = both_frames[..., channels:]
    cot_all = lax.all_to_all(cot_frames, "height", split_axis=3, concat_axis=1, tiled=True)

    window = lax.dynamic_slice(
        framed,
        (frame_index * frame_count, row_index * row_count, 0, 0),
        (frame_count + 2, row_count + 2, padded_cols, channels),
    )
    conv_out = forward_conv(window, weight_cube, row_count, col_count).reshape(
        frame_count, row_count, col_count, channels
    )
    output = (latent_wide + conv_out + bias).astype(jnp.bfloat16)

    weight_grad = block_weight_grad(framed, cot_all, frame_index, share_rows, channels) * inverse_root

    cot_future = lax.dynamic_slice_in_dim(
        jnp.pad(cot_frames, ((0, 2), (0, 0), (0, 0), (0, 0))), frame_index * frame_count, 3, 0
    )
    cotangent_edged = padded(cot_future, (("height", 1),), 1)
    future_block = jnp.pad(cotangent_edged, ((0, 0), (0, 0), (1, right_pad), (0, 0)))
    hidden_grad = backward_conv(future_block, weight_cube, row_count, col_count).reshape(frame_count, row_count, col_count, channels)
    sigmoid_pre = jax.nn.sigmoid(normed)
    normed_grad = hidden_grad * sigmoid_pre * (1.0 + normed * (1.0 - sigmoid_pre))
    scaled_grad = normed_grad * gain
    unit_latent = latent_wide / root_mean
    inner = jnp.mean(scaled_grad * unit_latent, axis=-1, keepdims=True)
    latent_grad = (
        cotangent.astype(jnp.float32) + (scaled_grad - unit_latent * inner) / root_mean
    ).astype(jnp.bfloat16)
    return (output, latent_grad, weight_grad)


def solution(mesh):
    placed = (
        P(("grp", "tm"), "height", None, None),
        P(),
        P(),
        P(),
        P(("grp", "tm"), "height", None, None),
    )
    return jax.shard_map(
        local,
        mesh=mesh,
        in_specs=placed,
        out_specs=(
            P(("grp", "tm"), "height", None, None),
            P(("grp", "tm"), "height", None, None),
            P(("grp", "tm"), "height"),
        ),
        check_vma=False,
    )
```

```python
import math

import jax
import jax.numpy as jnp
from jax import lax
from jax.sharding import PartitionSpec as P


def shifted_2(value, axis, by):
    devices = lax.axis_size(axis)
    pairs = [(i, i + by) for i in range(devices) if 0 <= i + by < devices]
    return lax.ppermute(value, axis, pairs)


def padded(cells, sides, width):
    for axis, dim in sides:
        count = lax.axis_size(axis)
        ends = count - 1
        head = lax.slice_in_dim(cells, 0, width, axis=dim)
        tail = lax.slice_in_dim(cells, cells.shape[dim] - width, cells.shape[dim], axis=dim)
        cells = jnp.concatenate(
            [
                lax.ppermute(tail, axis, [(i, (i + 1) % count) for i in range(ends)]),
                cells,
                lax.ppermute(head, axis, [((i + 1) % count, i) for i in range(ends)]),
            ],
            axis=dim,
        )
    return cells


def forward_arrange(cube):
    depth, rows_t, cols_t, inputs, outputs = cube.shape
    return cube.transpose(0, 1, 3, 2, 4).reshape(9, inputs, 3 * outputs)


def backward_arrange(cube):
    depth, rows_t, cols_t, inputs, outputs = cube.shape
    return cube.transpose(0, 1, 4, 2, 3).reshape(9, outputs, 3 * inputs)


def forward_conv(window, cube, row_total, col_total):
    window = window[:, :, : col_total + 2]
    result = lax.conv_general_dilated(
        window[None],
        cube,
        (1, 1, 1),
        "VALID",
        dimension_numbers=("NDHWC", "DHWIO", "NDHWC"),
        preferred_element_type=jnp.float32,
    )
    return result[0, 0]


def backward_conv(window, cube, row_total, col_total):
    window = window[:, :, : col_total + 2]
    result = lax.conv_general_dilated(
        window[None],
        jnp.flip(cube, (0, 1, 2)),
        (1, 1, 1),
        "VALID",
        dimension_numbers=("NDHWC", "DHWOI", "NDHWC"),
        preferred_element_type=jnp.float32,
    )
    return result[0, 0]


def pair_count(tap_rows, share_rows, pair_rows, parts):
    most = 1
    for index in range(parts):
        first = index * share_rows
        last = first + share_rows - 1
        most = max(most, last // pair_rows - first // pair_rows + 1)
    return most


def block_weight_grad(framed, cot_all, frame_index, share_rows, channels):
    frame_total, row_total, col_total, slots = cot_all.shape
    padded_cols = framed.shape[2]
    pair_rows = 3 * channels
    tap_rows = 27 * channels
    flat_count = frame_total * row_total * padded_cols
    shifted = jnp.stack(
        [
            jnp.pad(
                cot_all,
                ((0, 0), (0, 0), (col_tap, padded_cols - col_total - col_tap), (0, 0)),
            )
            for col_tap in range(3)
        ],
        axis=3,
    )
    first_row = frame_index * share_rows
    first_pair = first_row // pair_rows
    count = pair_count(tap_rows, share_rows, pair_rows, tap_rows // share_rows)
    pieces = []
    for step in range(count):
        pair = jnp.minimum(first_pair + step, 8)
        depth_tap = pair // 3
        row_tap = pair % 3
        slab = lax.dynamic_slice(
            framed,
            (depth_tap, row_tap, 0, 0),
            (frame_total, row_total, padded_cols, channels),
        )
        product = lax.dot_general(
            shifted, slab, (((0, 1, 2), (0, 1, 2)), ((), ())), preferred_element_type=jnp.float32
        )
        pieces.append(product.transpose(0, 2, 1).reshape(pair_rows, slots))
    stacked = jnp.concatenate(pieces, axis=0)
    return lax.dynamic_slice_in_dim(stacked, first_row - first_pair * pair_rows, share_rows, 0)


def gather_rows(own, height_count):
    frame_total, row_count, col_count, channels = own.shape
    height_index = lax.axis_index("height")
    core = height_index % 2
    chip = height_index // 2
    chips = height_count // 2
    first = core == 0
    sibling = [(i, i ^ 1) for i in range(height_count)]
    mine = [own] + [
        lax.ppermute(
            own, "height", [(i, (i + 2 * step) % height_count) for i in range(height_count)]
        )
        for step in range(1, chips)
    ]
    stacked = jnp.concatenate(mine, axis=1)
    twins = lax.ppermute(stacked, "height", sibling)
    source = jnp.concatenate([stacked, twins], axis=1)
    blocks = []
    for place in range(height_count):
        other = (place % 2 != core).astype(jnp.int32)
        index = other * chips + (chip - place // 2) % chips
        blocks.append(lax.dynamic_slice_in_dim(source, index * row_count, row_count, 1))
    return jnp.concatenate(blocks, axis=1)


def gather_frames(block):
    count = lax.axis_size("tm")
    position = lax.axis_index("tm")
    up = [(i, i + 1) for i in range(count - 1)]
    down = [(i + 1, i) for i in range(count - 1)]
    earlier, later = [], []
    rising, falling = block, block
    for step in range(1, count):
        rising = lax.ppermute(rising, "tm", up)
        falling = lax.ppermute(falling, "tm", down)
        earlier.append(rising)
        later.append(falling)
    relative = jnp.concatenate(earlier[::-1] + [block] + later, axis=0)
    return lax.dynamic_slice_in_dim(relative, count - 1 - position, count * block.shape[0], 0)


def local(latents, gain, bias, weight, cotangent):
    frame_count, row_count, col_count, channels = latents.shape
    latent_wide = latents.astype(jnp.float32)
    root_mean = jnp.sqrt(jnp.mean(latent_wide * latent_wide, axis=-1, keepdims=True) + 1e-06)
    normed = latent_wide / root_mean * gain
    hidden = jax.nn.silu(normed).astype(jnp.bfloat16)
    height_count = lax.axis_size("height")
    frame_devices = lax.axis_size("tm")
    frame_index = lax.axis_index("tm")
    row_index = lax.axis_index("height")
    total_rows = row_count * height_count
    total_frames = frame_count * frame_devices
    tap_rows = 27 * channels
    share_rows = tap_rows // frame_devices
    padded_cols = -(-(col_count + 2) // 8) * 8
    right_pad = padded_cols - col_count - 1
    inverse_root = 1.0 / math.sqrt(total_frames * total_rows * col_count)
    weight_cube = weight.reshape(3, 3, 3, channels, channels)

    both_frames = gather_frames(jnp.concatenate([hidden, cotangent], axis=-1))
    hidden_all = gather_rows(both_frames[..., :channels], height_count)
    framed = jnp.pad(hidden_all, ((2, 0), (1, 1), (1, right_pad), (0, 0)))

    cot_frames = both_frames[..., channels:]
    cot_all = lax.all_to_all(cot_frames, "height", split_axis=3, concat_axis=1, tiled=True)

    window = lax.dynamic_slice(
        framed,
        (frame_index * frame_count, row_index * row_count, 0, 0),
        (frame_count + 2, row_count + 2, padded_cols, channels),
    )
    conv_out = forward_conv(window, weight_cube, row_count, col_count).reshape(
        frame_count, row_count, col_count, channels
    )
    output = (latent_wide + conv_out + bias).astype(jnp.bfloat16)

    weight_grad = block_weight_grad(framed, cot_all, frame_index, share_rows, channels) * inverse_root

    cot_future = lax.dynamic_slice_in_dim(
        jnp.pad(cot_frames, ((0, 2), (0, 0), (0, 0), (0, 0))), frame_index * frame_count, 3, 0
    )
    cotangent_edged = padded(cot_future, (("height", 1),), 1)
    future_block = jnp.pad(cotangent_edged, ((0, 0), (0, 0), (1, right_pad), (0, 0)))
    hidden_grad = backward_conv(future_block, weight_cube, row_count, col_count).reshape(frame_count, row_count, col_count, channels)
    sigmoid_pre = jax.nn.sigmoid(normed)
    normed_grad = hidden_grad * sigmoid_pre * (1.0 + normed * (1.0 - sigmoid_pre))
    scaled_grad = normed_grad * gain
    unit_latent = latent_wide / root_mean
    inner = jnp.mean(scaled_grad * unit_latent, axis=-1, keepdims=True)
    latent_grad = (
        cotangent.astype(jnp.float32) + (scaled_grad - unit_latent * inner) / root_mean
    ).astype(jnp.bfloat16)
    return (output, latent_grad, weight_grad)


def solution(mesh):
    placed = (
        P(("grp", "tm"), "height", None, None),
        P(),
        P(),
        P(),
        P(("grp", "tm"), "height", None, None),
    )
    return jax.shard_map(
        local,
        mesh=mesh,
        in_specs=placed,
        out_specs=(
            P(("grp", "tm"), "height", None, None),
            P(("grp", "tm"), "height", None, None),
            P(("grp", "tm"), "height"),
        ),
        check_vma=False,
    )
```

```python
import math

import jax
import jax.numpy as jnp
from jax import lax
from jax.sharding import PartitionSpec as P


def shifted_2(value, axis, by):
    devices = lax.axis_size(axis)
    pairs = [(i, i + by) for i in range(devices) if 0 <= i + by < devices]
    return lax.ppermute(value, axis, pairs)


def padded(cells, sides, width):
    for axis, dim in sides:
        count = lax.axis_size(axis)
        ends = count - 1
        head = lax.slice_in_dim(cells, 0, width, axis=dim)
        tail = lax.slice_in_dim(cells, cells.shape[dim] - width, cells.shape[dim], axis=dim)
        cells = jnp.concatenate(
            [
                lax.ppermute(tail, axis, [(i, (i + 1) % count) for i in range(ends)]),
                cells,
                lax.ppermute(head, axis, [((i + 1) % count, i) for i in range(ends)]),
            ],
            axis=dim,
        )
    return cells


def forward_arrange(cube):
    depth, rows_t, cols_t, inputs, outputs = cube.shape
    return cube.transpose(0, 1, 3, 2, 4).reshape(9, inputs, 3 * outputs)


def backward_arrange(cube):
    depth, rows_t, cols_t, inputs, outputs = cube.shape
    return cube.transpose(0, 1, 4, 2, 3).reshape(9, outputs, 3 * inputs)


def forward_conv(window, cube, row_total, col_total):
    window = window[:, :, : col_total + 2]
    result = lax.conv_general_dilated(
        window[None],
        cube,
        (1, 1, 1),
        "VALID",
        dimension_numbers=("NDHWC", "DHWIO", "NDHWC"),
        preferred_element_type=jnp.float32,
    )
    return result[0, 0]


def backward_conv(window, cube, row_total, col_total):
    window = window[:, :, : col_total + 2]
    result = lax.conv_general_dilated(
        window[None],
        jnp.flip(cube, (0, 1, 2)),
        (1, 1, 1),
        "VALID",
        dimension_numbers=("NDHWC", "DHWOI", "NDHWC"),
        preferred_element_type=jnp.float32,
    )
    return result[0, 0]


def pair_count(tap_rows, share_rows, pair_rows, parts):
    most = 1
    for index in range(parts):
        first = index * share_rows
        last = first + share_rows - 1
        most = max(most, last // pair_rows - first // pair_rows + 1)
    return most


def block_weight_grad(hidden_all, cot_all, frame_index, share_rows, channels):
    frame_total, row_total, col_total, slots = cot_all.shape
    pair_rows = 3 * channels
    tap_rows = 27 * channels
    edged = jnp.pad(cot_all, ((0, 2), (1, 1), (1, 1), (0, 0)))
    shifted = jnp.stack(
        [edged[:, :, 2 - col_tap : 2 - col_tap + col_total] for col_tap in range(3)], axis=3
    )
    first_row = frame_index * share_rows
    first_pair = first_row // pair_rows
    count = pair_count(tap_rows, share_rows, pair_rows, tap_rows // share_rows)
    pieces = []
    for step in range(count):
        pair = jnp.minimum(first_pair + step, 8)
        depth_tap = pair // 3
        row_tap = pair % 3
        window = lax.dynamic_slice(
            shifted,
            (2 - depth_tap, 2 - row_tap, 0, 0, 0),
            (frame_total, row_total, col_total, 3, slots),
        )
        product = lax.dot_general(
            window, hidden_all, (((0, 1, 2), (0, 1, 2)), ((), ())),
            preferred_element_type=jnp.float32,
        )
        pieces.append(product.transpose(0, 2, 1).reshape(pair_rows, slots))
    stacked = jnp.concatenate(pieces, axis=0)
    return lax.dynamic_slice_in_dim(stacked, first_row - first_pair * pair_rows, share_rows, 0)


def gather_rows(own, height_count):
    frame_total, row_count, col_count, channels = own.shape
    height_index = lax.axis_index("height")
    core = height_index % 2
    chip = height_index // 2
    chips = height_count // 2
    first = core == 0
    sibling = [(i, i ^ 1) for i in range(height_count)]
    mine = [own] + [
        lax.ppermute(
            own, "height", [(i, (i + 2 * step) % height_count) for i in range(height_count)]
        )
        for step in range(1, chips)
    ]
    stacked = jnp.concatenate(mine, axis=1)
    twins = lax.ppermute(stacked, "height", sibling)
    block = 2 * row_count
    relative = []
    for step in reversed(range(chips)):
        ours = stacked[:, step * row_count : (step + 1) * row_count]
        theirs = twins[:, step * row_count : (step + 1) * row_count]
        relative.append(
            jnp.where(
                first,
                jnp.concatenate([ours, theirs], axis=1),
                jnp.concatenate([theirs, ours], axis=1),
            )
        )
    relative = jnp.concatenate(relative, axis=1)
    return jnp.concatenate(
        [
            lax.dynamic_slice_in_dim(relative, ((place - chip - 1) % chips) * block, block, 1)
            for place in range(chips)
        ],
        axis=1,
    )


def gather_frames(block):
    count = lax.axis_size("tm")
    position = lax.axis_index("tm")
    up = [(i, i + 1) for i in range(count - 1)]
    down = [(i + 1, i) for i in range(count - 1)]
    earlier, later = [], []
    rising, falling = block, block
    for step in range(1, count):
        rising = lax.ppermute(rising, "tm", up)
        falling = lax.ppermute(falling, "tm", down)
        earlier.append(rising)
        later.append(falling)
    relative = jnp.concatenate(earlier[::-1] + [block] + later, axis=0)
    return lax.dynamic_slice_in_dim(relative, count - 1 - position, count * block.shape[0], 0)


def local(latents, gain, bias, weight, cotangent):
    frame_count, row_count, col_count, channels = latents.shape
    latent_wide = latents.astype(jnp.float32)
    root_mean = jnp.sqrt(jnp.mean(latent_wide * latent_wide, axis=-1, keepdims=True) + 1e-06)
    normed = latent_wide / root_mean * gain
    hidden = jax.nn.silu(normed).astype(jnp.bfloat16)
    height_count = lax.axis_size("height")
    frame_devices = lax.axis_size("tm")
    frame_index = lax.axis_index("tm")
    row_index = lax.axis_index("height")
    total_rows = row_count * height_count
    total_frames = frame_count * frame_devices
    tap_rows = 27 * channels
    share_rows = tap_rows // frame_devices
    padded_cols = -(-(col_count + 2) // 8) * 8
    right_pad = padded_cols - col_count - 1
    inverse_root = 1.0 / math.sqrt(total_frames * total_rows * col_count)
    weight_cube = weight.reshape(3, 3, 3, channels, channels)

    both_frames = gather_frames(jnp.concatenate([hidden, cotangent], axis=-1))
    hidden_all = gather_rows(both_frames[..., :channels], height_count)

    cot_frames = both_frames[..., channels:]
    cot_all = lax.all_to_all(cot_frames, "height", split_axis=3, concat_axis=1, tiled=True)

    window = lax.dynamic_slice(
        jnp.pad(hidden_all, ((2, 0), (1, 1), (1, 1), (0, 0))),
        (frame_index * frame_count, row_index * row_count, 0, 0),
        (frame_count + 2, row_count + 2, col_count + 2, channels),
    )
    conv_out = forward_conv(window, weight_cube, row_count, col_count).reshape(
        frame_count, row_count, col_count, channels
    )
    output = (latent_wide + conv_out + bias).astype(jnp.bfloat16)

    weight_grad = (
        block_weight_grad(hidden_all, cot_all, frame_index, share_rows, channels) * inverse_root
    )

    cot_future = lax.dynamic_slice_in_dim(
        jnp.pad(cot_frames, ((0, 2), (0, 0), (0, 0), (0, 0))), frame_index * frame_count, 3, 0
    )
    cotangent_edged = padded(cot_future, (("height", 1),), 1)
    future_block = jnp.pad(cotangent_edged, ((0, 0), (0, 0), (1, right_pad), (0, 0)))
    hidden_grad = backward_conv(future_block, weight_cube, row_count, col_count).reshape(frame_count, row_count, col_count, channels)
    sigmoid_pre = jax.nn.sigmoid(normed)
    normed_grad = hidden_grad * sigmoid_pre * (1.0 + normed * (1.0 - sigmoid_pre))
    scaled_grad = normed_grad * gain
    unit_latent = latent_wide / root_mean
    inner = jnp.mean(scaled_grad * unit_latent, axis=-1, keepdims=True)
    latent_grad = (
        cotangent.astype(jnp.float32) + (scaled_grad - unit_latent * inner) / root_mean
    ).astype(jnp.bfloat16)
    return (output, latent_grad, weight_grad)


def solution(mesh):
    placed = (
        P(("grp", "tm"), "height", None, None),
        P(),
        P(),
        P(),
        P(("grp", "tm"), "height", None, None),
    )
    return jax.shard_map(
        local,
        mesh=mesh,
        in_specs=placed,
        out_specs=(
            P(("grp", "tm"), "height", None, None),
            P(("grp", "tm"), "height", None, None),
            P(("grp", "tm"), "height"),
        ),
        check_vma=False,
    )
```

```python
import math

import jax
import jax.numpy as jnp
from jax import lax
from jax.sharding import PartitionSpec as P


def shifted_2(value, axis, by):
    devices = lax.axis_size(axis)
    pairs = [(i, i + by) for i in range(devices) if 0 <= i + by < devices]
    return lax.ppermute(value, axis, pairs)


def padded(cells, sides, width):
    for axis, dim in sides:
        count = lax.axis_size(axis)
        ends = count - 1
        head = lax.slice_in_dim(cells, 0, width, axis=dim)
        tail = lax.slice_in_dim(cells, cells.shape[dim] - width, cells.shape[dim], axis=dim)
        cells = jnp.concatenate(
            [
                lax.ppermute(tail, axis, [(i, (i + 1) % count) for i in range(ends)]),
                cells,
                lax.ppermute(head, axis, [((i + 1) % count, i) for i in range(ends)]),
            ],
            axis=dim,
        )
    return cells


def forward_arrange(cube):
    depth, rows_t, cols_t, inputs, outputs = cube.shape
    return cube.transpose(0, 1, 3, 2, 4).reshape(9, inputs, 3 * outputs)


def backward_arrange(cube):
    depth, rows_t, cols_t, inputs, outputs = cube.shape
    return cube.transpose(0, 1, 4, 2, 3).reshape(9, outputs, 3 * inputs)


def forward_conv(window, cube, row_total, col_total):
    window = window[:, :, : col_total + 2]
    result = lax.conv_general_dilated(
        window[None],
        cube,
        (1, 1, 1),
        "VALID",
        dimension_numbers=("NDHWC", "DHWIO", "NDHWC"),
        preferred_element_type=jnp.float32,
    )
    return result[0, 0]


def backward_conv(window, cube, row_total, col_total):
    window = window[:, :, : col_total + 2]
    result = lax.conv_general_dilated(
        window[None],
        jnp.flip(cube, (0, 1, 2)),
        (1, 1, 1),
        "VALID",
        dimension_numbers=("NDHWC", "DHWOI", "NDHWC"),
        preferred_element_type=jnp.float32,
    )
    return result[0, 0]


def pair_count(tap_rows, share_rows, pair_rows, parts):
    most = 1
    for index in range(parts):
        first = index * share_rows
        last = first + share_rows - 1
        most = max(most, last // pair_rows - first // pair_rows + 1)
    return most


def block_weight_grad(hidden_all, cot_all, frame_index, share_rows, channels):
    frame_total, row_total, col_total, slots = cot_all.shape
    pair_rows = 3 * channels
    tap_rows = 27 * channels
    edged = jnp.pad(cot_all, ((0, 2), (1, 1), (1, 1), (0, 0)))
    shifted = jnp.stack(
        [edged[:, :, 2 - col_tap : 2 - col_tap + col_total] for col_tap in range(3)], axis=3
    )
    first_row = frame_index * share_rows
    first_pair = first_row // pair_rows
    count = pair_count(tap_rows, share_rows, pair_rows, tap_rows // share_rows)
    pieces = []
    for step in range(count):
        pair = jnp.minimum(first_pair + step, 8)
        depth_tap = pair // 3
        row_tap = pair % 3
        window = lax.dynamic_slice(
            shifted,
            (2 - depth_tap, 2 - row_tap, 0, 0, 0),
            (frame_total, row_total, col_total, 3, slots),
        )
        product = lax.dot_general(
            window, hidden_all, (((0, 1, 2), (0, 1, 2)), ((), ())),
            preferred_element_type=jnp.float32,
        )
        pieces.append(product.transpose(0, 2, 1).reshape(pair_rows, slots))
    stacked = jnp.concatenate(pieces, axis=0)
    return lax.dynamic_slice_in_dim(stacked, first_row - first_pair * pair_rows, share_rows, 0)


def gather_rows(own, height_count):
    frame_total, row_count, col_count, channels = own.shape
    height_index = lax.axis_index("height")
    core = height_index % 2
    chip = height_index // 2
    chips = height_count // 2
    first = core == 0
    sibling = [(i, i ^ 1) for i in range(height_count)]
    mine = [own] + [
        lax.ppermute(
            own, "height", [(i, (i + 2 * step) % height_count) for i in range(height_count)]
        )
        for step in range(1, chips)
    ]
    stacked = jnp.concatenate(mine, axis=1)
    twins = lax.ppermute(stacked, "height", sibling)
    block = 2 * row_count
    relative = []
    for step in reversed(range(chips)):
        ours = stacked[:, step * row_count : (step + 1) * row_count]
        theirs = twins[:, step * row_count : (step + 1) * row_count]
        relative.append(
            jnp.where(
                first,
                jnp.concatenate([ours, theirs], axis=1),
                jnp.concatenate([theirs, ours], axis=1),
            )
        )
    relative = jnp.concatenate(relative, axis=1)
    return jnp.concatenate(
        [
            lax.dynamic_slice_in_dim(relative, ((place - chip - 1) % chips) * block, block, 1)
            for place in range(chips)
        ],
        axis=1,
    )


def gather_frames(block):
    count = lax.axis_size("tm")
    position = lax.axis_index("tm")
    up = [(i, i + 1) for i in range(count - 1)]
    down = [(i + 1, i) for i in range(count - 1)]
    earlier, later = [], []
    rising, falling = block, block
    for step in range(1, count):
        rising = lax.ppermute(rising, "tm", up)
        falling = lax.ppermute(falling, "tm", down)
        earlier.append(rising)
        later.append(falling)
    relative = jnp.concatenate(earlier[::-1] + [block] + later, axis=0)
    return lax.dynamic_slice_in_dim(relative, count - 1 - position, count * block.shape[0], 0)


def local(latents, gain, bias, weight, cotangent):
    frame_count, row_count, col_count, channels = latents.shape
    latent_wide = latents.astype(jnp.float32)
    root_mean = jnp.sqrt(jnp.mean(latent_wide * latent_wide, axis=-1, keepdims=True) + 1e-06)
    normed = latent_wide / root_mean * gain
    hidden = jax.nn.silu(normed).astype(jnp.bfloat16)
    height_count = lax.axis_size("height")
    frame_devices = lax.axis_size("tm")
    frame_index = lax.axis_index("tm")
    row_index = lax.axis_index("height")
    total_rows = row_count * height_count
    total_frames = frame_count * frame_devices
    tap_rows = 27 * channels
    share_rows = tap_rows // frame_devices
    padded_cols = -(-(col_count + 2) // 8) * 8
    right_pad = padded_cols - col_count - 1
    inverse_root = 1.0 / math.sqrt(total_frames * total_rows * col_count)
    weight_cube = weight.reshape(3, 3, 3, channels, channels)

    hidden_all = gather_rows(gather_frames(hidden), height_count)

    cot_frames = gather_frames(cotangent)
    cot_all = lax.all_to_all(cot_frames, "height", split_axis=3, concat_axis=1, tiled=True)

    window = lax.dynamic_slice(
        jnp.pad(hidden_all, ((2, 0), (1, 1), (1, 1), (0, 0))),
        (frame_index * frame_count, row_index * row_count, 0, 0),
        (frame_count + 2, row_count + 2, col_count + 2, channels),
    )
    conv_out = forward_conv(window, weight_cube, row_count, col_count).reshape(
        frame_count, row_count, col_count, channels
    )
    output = (latent_wide + conv_out + bias).astype(jnp.bfloat16)

    weight_grad = (
        block_weight_grad(hidden_all, cot_all, frame_index, share_rows, channels) * inverse_root
    )

    cot_future = lax.dynamic_slice_in_dim(
        jnp.pad(cot_frames, ((0, 2), (0, 0), (0, 0), (0, 0))), frame_index * frame_count, 3, 0
    )
    cotangent_edged = padded(cot_future, (("height", 1),), 1)
    future_block = jnp.pad(cotangent_edged, ((0, 0), (0, 0), (1, right_pad), (0, 0)))
    hidden_grad = backward_conv(future_block, weight_cube, row_count, col_count).reshape(frame_count, row_count, col_count, channels)
    sigmoid_pre = jax.nn.sigmoid(normed)
    normed_grad = hidden_grad * sigmoid_pre * (1.0 + normed * (1.0 - sigmoid_pre))
    scaled_grad = normed_grad * gain
    unit_latent = latent_wide / root_mean
    inner = jnp.mean(scaled_grad * unit_latent, axis=-1, keepdims=True)
    latent_grad = (
        cotangent.astype(jnp.float32) + (scaled_grad - unit_latent * inner) / root_mean
    ).astype(jnp.bfloat16)
    return (output, latent_grad, weight_grad)


def solution(mesh):
    placed = (
        P(("grp", "tm"), "height", None, None),
        P(),
        P(),
        P(),
        P(("grp", "tm"), "height", None, None),
    )
    return jax.shard_map(
        local,
        mesh=mesh,
        in_specs=placed,
        out_specs=(
            P(("grp", "tm"), "height", None, None),
            P(("grp", "tm"), "height", None, None),
            P(("grp", "tm"), "height"),
        ),
        check_vma=False,
    )
```

```python
import math

import jax
import jax.numpy as jnp
from jax import lax
from jax.sharding import PartitionSpec as P


def shifted_2(value, axis, by):
    devices = lax.axis_size(axis)
    pairs = [(i, i + by) for i in range(devices) if 0 <= i + by < devices]
    return lax.ppermute(value, axis, pairs)


def padded(cells, sides, width):
    for axis, dim in sides:
        count = lax.axis_size(axis)
        ends = count - 1
        head = lax.slice_in_dim(cells, 0, width, axis=dim)
        tail = lax.slice_in_dim(cells, cells.shape[dim] - width, cells.shape[dim], axis=dim)
        cells = jnp.concatenate(
            [
                lax.ppermute(tail, axis, [(i, (i + 1) % count) for i in range(ends)]),
                cells,
                lax.ppermute(head, axis, [((i + 1) % count, i) for i in range(ends)]),
            ],
            axis=dim,
        )
    return cells


def forward_arrange(cube):
    depth, rows_t, cols_t, inputs, outputs = cube.shape
    return cube.transpose(0, 1, 3, 2, 4).reshape(9, inputs, 3 * outputs)


def backward_arrange(cube):
    depth, rows_t, cols_t, inputs, outputs = cube.shape
    return cube.transpose(0, 1, 4, 2, 3).reshape(9, outputs, 3 * inputs)


def forward_conv(window, cube, row_total, col_total):
    window = window[:, :, : col_total + 2]
    result = lax.conv_general_dilated(
        window[None],
        cube,
        (1, 1, 1),
        "VALID",
        dimension_numbers=("NDHWC", "DHWIO", "NDHWC"),
        preferred_element_type=jnp.float32,
    )
    return result[0, 0]


def backward_conv(window, cube, row_total, col_total):
    window = window[:, :, : col_total + 2]
    result = lax.conv_general_dilated(
        window[None],
        jnp.flip(cube, (0, 1, 2)),
        (1, 1, 1),
        "VALID",
        dimension_numbers=("NDHWC", "DHWOI", "NDHWC"),
        preferred_element_type=jnp.float32,
    )
    return result[0, 0]


def pair_count(tap_rows, share_rows, pair_rows, parts):
    most = 1
    for index in range(parts):
        first = index * share_rows
        last = first + share_rows - 1
        most = max(most, last // pair_rows - first // pair_rows + 1)
    return most


def block_weight_grad(hidden_all, cot_all, frame_index, share_rows, channels):
    frame_total, row_total, col_total, slots = cot_all.shape
    pair_rows = 3 * channels
    tap_rows = 27 * channels
    edged = jnp.pad(cot_all, ((0, 2), (1, 1), (1, 1), (0, 0)))
    shifted = jnp.stack(
        [edged[:, :, 2 - col_tap : 2 - col_tap + col_total] for col_tap in range(3)], axis=3
    )
    first_row = frame_index * share_rows
    first_pair = first_row // pair_rows
    count = pair_count(tap_rows, share_rows, pair_rows, tap_rows // share_rows)
    pieces = []
    for step in range(count):
        pair = jnp.minimum(first_pair + step, 8)
        depth_tap = pair // 3
        row_tap = pair % 3
        window = lax.dynamic_slice(
            shifted,
            (2 - depth_tap, 2 - row_tap, 0, 0, 0),
            (frame_total, row_total, col_total, 3, slots),
        )
        product = lax.dot_general(
            window, hidden_all, (((0, 1, 2), (0, 1, 2)), ((), ())),
            preferred_element_type=jnp.float32,
        )
        pieces.append(product.transpose(0, 2, 1).reshape(pair_rows, slots))
    stacked = jnp.concatenate(pieces, axis=0)
    return lax.dynamic_slice_in_dim(stacked, first_row - first_pair * pair_rows, share_rows, 0)


def gather_rows(own, height_count):
    frame_total, row_count, col_count, channels = own.shape
    height_index = lax.axis_index("height")
    core = height_index % 2
    chip = height_index // 2
    chips = height_count // 2
    first = core == 0
    sibling = [(i, i ^ 1) for i in range(height_count)]
    mine = [own] + [
        lax.ppermute(
            own, "height", [(i, (i + 2 * step) % height_count) for i in range(height_count)]
        )
        for step in range(1, chips)
    ]
    stacked = jnp.concatenate(mine, axis=1)
    twins = lax.ppermute(stacked, "height", sibling)
    block = 2 * row_count
    relative = []
    for step in reversed(range(chips)):
        ours = stacked[:, step * row_count : (step + 1) * row_count]
        theirs = twins[:, step * row_count : (step + 1) * row_count]
        relative.append(
            jnp.where(
                first,
                jnp.concatenate([ours, theirs], axis=1),
                jnp.concatenate([theirs, ours], axis=1),
            )
        )
    relative = jnp.concatenate(relative, axis=1)
    return jnp.concatenate(
        [
            lax.dynamic_slice_in_dim(relative, ((place - chip - 1) % chips) * block, block, 1)
            for place in range(chips)
        ],
        axis=1,
    )


def gather_frames(block):
    count = lax.axis_size("tm")
    copies = jnp.broadcast_to(block[None], (count,) + block.shape)
    frames = lax.all_to_all(copies, "tm", split_axis=0, concat_axis=0, tiled=True)
    return frames.reshape((count * block.shape[0],) + block.shape[1:])


def local(latents, gain, bias, weight, cotangent):
    frame_count, row_count, col_count, channels = latents.shape
    latent_wide = latents.astype(jnp.float32)
    root_mean = jnp.sqrt(jnp.mean(latent_wide * latent_wide, axis=-1, keepdims=True) + 1e-06)
    normed = latent_wide / root_mean * gain
    hidden = jax.nn.silu(normed).astype(jnp.bfloat16)
    height_count = lax.axis_size("height")
    frame_devices = lax.axis_size("tm")
    frame_index = lax.axis_index("tm")
    row_index = lax.axis_index("height")
    total_rows = row_count * height_count
    total_frames = frame_count * frame_devices
    tap_rows = 27 * channels
    share_rows = tap_rows // frame_devices
    padded_cols = -(-(col_count + 2) // 8) * 8
    right_pad = padded_cols - col_count - 1
    inverse_root = 1.0 / math.sqrt(total_frames * total_rows * col_count)
    weight_cube = weight.reshape(3, 3, 3, channels, channels)

    both_frames = gather_frames(jnp.concatenate([hidden, cotangent], axis=-1))
    hidden_all = gather_rows(both_frames[..., :channels], height_count)

    cot_frames = both_frames[..., channels:]
    cot_all = lax.all_to_all(cot_frames, "height", split_axis=3, concat_axis=1, tiled=True)

    window = lax.dynamic_slice(
        jnp.pad(hidden_all, ((2, 0), (1, 1), (1, 1), (0, 0))),
        (frame_index * frame_count, row_index * row_count, 0, 0),
        (frame_count + 2, row_count + 2, col_count + 2, channels),
    )
    conv_out = forward_conv(window, weight_cube, row_count, col_count).reshape(
        frame_count, row_count, col_count, channels
    )
    output = (latent_wide + conv_out + bias).astype(jnp.bfloat16)

    weight_grad = (
        block_weight_grad(hidden_all, cot_all, frame_index, share_rows, channels) * inverse_root
    )

    cot_future = lax.dynamic_slice_in_dim(
        jnp.pad(cot_frames, ((0, 2), (0, 0), (0, 0), (0, 0))), frame_index * frame_count, 3, 0
    )
    cotangent_edged = padded(cot_future, (("height", 1),), 1)
    future_block = jnp.pad(cotangent_edged, ((0, 0), (0, 0), (1, right_pad), (0, 0)))
    hidden_grad = backward_conv(future_block, weight_cube, row_count, col_count).reshape(frame_count, row_count, col_count, channels)
    sigmoid_pre = jax.nn.sigmoid(normed)
    normed_grad = hidden_grad * sigmoid_pre * (1.0 + normed * (1.0 - sigmoid_pre))
    scaled_grad = normed_grad * gain
    unit_latent = latent_wide / root_mean
    inner = jnp.mean(scaled_grad * unit_latent, axis=-1, keepdims=True)
    latent_grad = (
        cotangent.astype(jnp.float32) + (scaled_grad - unit_latent * inner) / root_mean
    ).astype(jnp.bfloat16)
    return (output, latent_grad, weight_grad)


def solution(mesh):
    placed = (
        P(("grp", "tm"), "height", None, None),
        P(),
        P(),
        P(),
        P(("grp", "tm"), "height", None, None),
    )
    return jax.shard_map(
        local,
        mesh=mesh,
        in_specs=placed,
        out_specs=(
            P(("grp", "tm"), "height", None, None),
            P(("grp", "tm"), "height", None, None),
            P(("grp", "tm"), "height"),
        ),
        check_vma=False,
    )
```

```python
import math

import jax
import jax.numpy as jnp
from jax import lax
from jax.sharding import PartitionSpec as P


def shifted_2(value, axis, by):
    devices = lax.axis_size(axis)
    pairs = [(i, i + by) for i in range(devices) if 0 <= i + by < devices]
    return lax.ppermute(value, axis, pairs)


def padded(cells, sides, width):
    for axis, dim in sides:
        count = lax.axis_size(axis)
        ends = count - 1
        head = lax.slice_in_dim(cells, 0, width, axis=dim)
        tail = lax.slice_in_dim(cells, cells.shape[dim] - width, cells.shape[dim], axis=dim)
        cells = jnp.concatenate(
            [
                lax.ppermute(tail, axis, [(i, (i + 1) % count) for i in range(ends)]),
                cells,
                lax.ppermute(head, axis, [((i + 1) % count, i) for i in range(ends)]),
            ],
            axis=dim,
        )
    return cells


def forward_arrange(cube):
    depth, rows_t, cols_t, inputs, outputs = cube.shape
    return cube.transpose(0, 1, 3, 2, 4).reshape(9, inputs, 3 * outputs)


def backward_arrange(cube):
    depth, rows_t, cols_t, inputs, outputs = cube.shape
    return cube.transpose(0, 1, 4, 2, 3).reshape(9, outputs, 3 * inputs)


def forward_conv(window, cube, row_total, col_total):
    window = window[:, :, : col_total + 2]
    result = lax.conv_general_dilated(
        window[None],
        cube,
        (1, 1, 1),
        "VALID",
        dimension_numbers=("NDHWC", "DHWIO", "NDHWC"),
        preferred_element_type=jnp.float32,
    )
    return result[0, 0]


def backward_conv(window, cube, row_total, col_total):
    window = window[:, :, : col_total + 2]
    result = lax.conv_general_dilated(
        window[None],
        jnp.flip(cube, (0, 1, 2)),
        (1, 1, 1),
        "VALID",
        dimension_numbers=("NDHWC", "DHWOI", "NDHWC"),
        preferred_element_type=jnp.float32,
    )
    return result[0, 0]


def pair_count(tap_rows, share_rows, pair_rows, parts):
    most = 1
    for index in range(parts):
        first = index * share_rows
        last = first + share_rows - 1
        most = max(most, last // pair_rows - first // pair_rows + 1)
    return most


def block_weight_grad(hidden_all, cot_all, frame_index, share_rows, channels):
    frame_total, row_total, col_total, slots = cot_all.shape
    pair_rows = 3 * channels
    tap_rows = 27 * channels
    edged = jnp.pad(cot_all, ((0, 2), (1, 1), (1, 1), (0, 0)))
    shifted = jnp.stack(
        [edged[:, :, 2 - col_tap : 2 - col_tap + col_total] for col_tap in range(3)], axis=3
    )
    first_row = frame_index * share_rows
    first_pair = first_row // pair_rows
    count = pair_count(tap_rows, share_rows, pair_rows, tap_rows // share_rows)
    pieces = []
    for step in range(count):
        pair = jnp.minimum(first_pair + step, 8)
        depth_tap = pair // 3
        row_tap = pair % 3
        window = lax.dynamic_slice(
            shifted,
            (2 - depth_tap, 2 - row_tap, 0, 0, 0),
            (frame_total, row_total, col_total, 3, slots),
        )
        product = lax.dot_general(
            window, hidden_all, (((0, 1, 2), (0, 1, 2)), ((), ())),
            preferred_element_type=jnp.float32,
        )
        pieces.append(product.transpose(0, 2, 1).reshape(pair_rows, slots))
    stacked = jnp.concatenate(pieces, axis=0)
    return lax.dynamic_slice_in_dim(stacked, first_row - first_pair * pair_rows, share_rows, 0)


def gather_rows(own, height_count):
    frame_total, row_count, col_count, channels = own.shape
    height_index = lax.axis_index("height")
    core = height_index % 2
    chip = height_index // 2
    chips = height_count // 2
    first = core == 0
    sibling = [(i, i ^ 1) for i in range(height_count)]
    mine = [own] + [
        lax.ppermute(
            own, "height", [(i, (i + 2 * step) % height_count) for i in range(height_count)]
        )
        for step in range(1, chips)
    ]
    stacked = jnp.concatenate(mine, axis=1)
    twins = jnp.concatenate(
        [lax.ppermute(own, "height", sibling)]
        + ([lax.ppermute(stacked[:, row_count:], "height", sibling)] if chips > 1 else []),
        axis=1,
    )
    block = 2 * row_count
    relative = []
    for step in reversed(range(chips)):
        ours = stacked[:, step * row_count : (step + 1) * row_count]
        theirs = twins[:, step * row_count : (step + 1) * row_count]
        relative.append(
            jnp.where(
                first,
                jnp.concatenate([ours, theirs], axis=1),
                jnp.concatenate([theirs, ours], axis=1),
            )
        )
    relative = jnp.concatenate(relative, axis=1)
    return jnp.concatenate(
        [
            lax.dynamic_slice_in_dim(relative, ((place - chip - 1) % chips) * block, block, 1)
            for place in range(chips)
        ],
        axis=1,
    )


def gather_frames(block):
    count = lax.axis_size("tm")
    position = lax.axis_index("tm")
    up = [(i, i + 1) for i in range(count - 1)]
    down = [(i + 1, i) for i in range(count - 1)]
    earlier, later = [], []
    rising, falling = block, block
    for step in range(1, count):
        rising = lax.ppermute(rising, "tm", up)
        falling = lax.ppermute(falling, "tm", down)
        earlier.append(rising)
        later.append(falling)
    relative = jnp.concatenate(earlier[::-1] + [block] + later, axis=0)
    return lax.dynamic_slice_in_dim(relative, count - 1 - position, count * block.shape[0], 0)


def local(latents, gain, bias, weight, cotangent):
    frame_count, row_count, col_count, channels = latents.shape
    latent_wide = latents.astype(jnp.float32)
    root_mean = jnp.sqrt(jnp.mean(latent_wide * latent_wide, axis=-1, keepdims=True) + 1e-06)
    normed = latent_wide / root_mean * gain
    hidden = jax.nn.silu(normed).astype(jnp.bfloat16)
    height_count = lax.axis_size("height")
    frame_devices = lax.axis_size("tm")
    frame_index = lax.axis_index("tm")
    row_index = lax.axis_index("height")
    total_rows = row_count * height_count
    total_frames = frame_count * frame_devices
    tap_rows = 27 * channels
    share_rows = tap_rows // frame_devices
    padded_cols = -(-(col_count + 2) // 8) * 8
    right_pad = padded_cols - col_count - 1
    inverse_root = 1.0 / math.sqrt(total_frames * total_rows * col_count)
    weight_cube = weight.reshape(3, 3, 3, channels, channels)

    both_frames = gather_frames(jnp.concatenate([hidden, cotangent], axis=-1))
    hidden_all = gather_rows(both_frames[..., :channels], height_count)

    cot_frames = both_frames[..., channels:]
    cot_all = lax.all_to_all(cot_frames, "height", split_axis=3, concat_axis=1, tiled=True)

    window = lax.dynamic_slice(
        jnp.pad(hidden_all, ((2, 0), (1, 1), (1, 1), (0, 0))),
        (frame_index * frame_count, row_index * row_count, 0, 0),
        (frame_count + 2, row_count + 2, col_count + 2, channels),
    )
    conv_out = forward_conv(window, weight_cube, row_count, col_count).reshape(
        frame_count, row_count, col_count, channels
    )
    output = (latent_wide + conv_out + bias).astype(jnp.bfloat16)

    weight_grad = (
        block_weight_grad(hidden_all, cot_all, frame_index, share_rows, channels) * inverse_root
    )

    cot_future = lax.dynamic_slice_in_dim(
        jnp.pad(cot_frames, ((0, 2), (0, 0), (0, 0), (0, 0))), frame_index * frame_count, 3, 0
    )
    cotangent_edged = padded(cot_future, (("height", 1),), 1)
    future_block = jnp.pad(cotangent_edged, ((0, 0), (0, 0), (1, right_pad), (0, 0)))
    hidden_grad = backward_conv(future_block, weight_cube, row_count, col_count).reshape(frame_count, row_count, col_count, channels)
    sigmoid_pre = jax.nn.sigmoid(normed)
    normed_grad = hidden_grad * sigmoid_pre * (1.0 + normed * (1.0 - sigmoid_pre))
    scaled_grad = normed_grad * gain
    unit_latent = latent_wide / root_mean
    inner = jnp.mean(scaled_grad * unit_latent, axis=-1, keepdims=True)
    latent_grad = (
        cotangent.astype(jnp.float32) + (scaled_grad - unit_latent * inner) / root_mean
    ).astype(jnp.bfloat16)
    return (output, latent_grad, weight_grad)


def solution(mesh):
    placed = (
        P(("grp", "tm"), "height", None, None),
        P(),
        P(),
        P(),
        P(("grp", "tm"), "height", None, None),
    )
    return jax.shard_map(
        local,
        mesh=mesh,
        in_specs=placed,
        out_specs=(
            P(("grp", "tm"), "height", None, None),
            P(("grp", "tm"), "height", None, None),
            P(("grp", "tm"), "height"),
        ),
        check_vma=False,
    )
```

```python
import math

import jax
import jax.numpy as jnp
from jax import lax
from jax.sharding import PartitionSpec as P


def shifted_2(value, axis, by):
    devices = lax.axis_size(axis)
    pairs = [(i, i + by) for i in range(devices) if 0 <= i + by < devices]
    return lax.ppermute(value, axis, pairs)


def padded(cells, sides, width):
    for axis, dim in sides:
        count = lax.axis_size(axis)
        ends = count - 1
        head = lax.slice_in_dim(cells, 0, width, axis=dim)
        tail = lax.slice_in_dim(cells, cells.shape[dim] - width, cells.shape[dim], axis=dim)
        cells = jnp.concatenate(
            [
                lax.ppermute(tail, axis, [(i, (i + 1) % count) for i in range(ends)]),
                cells,
                lax.ppermute(head, axis, [((i + 1) % count, i) for i in range(ends)]),
            ],
            axis=dim,
        )
    return cells


def forward_arrange(cube):
    depth, rows_t, cols_t, inputs, outputs = cube.shape
    return cube.transpose(0, 1, 3, 2, 4).reshape(9, inputs, 3 * outputs)


def backward_arrange(cube):
    depth, rows_t, cols_t, inputs, outputs = cube.shape
    return cube.transpose(0, 1, 4, 2, 3).reshape(9, outputs, 3 * inputs)


def forward_conv(window, cube, row_total, col_total):
    window = window[:, :, : col_total + 2]
    result = lax.conv_general_dilated(
        window[None],
        cube,
        (1, 1, 1),
        "VALID",
        dimension_numbers=("NDHWC", "DHWIO", "NDHWC"),
        preferred_element_type=jnp.float32,
    )
    return result[0, 0]


def backward_conv(window, cube, row_total, col_total):
    window = window[:, :, : col_total + 2]
    result = lax.conv_general_dilated(
        window[None],
        jnp.flip(cube, (0, 1, 2)),
        (1, 1, 1),
        "VALID",
        dimension_numbers=("NDHWC", "DHWOI", "NDHWC"),
        preferred_element_type=jnp.float32,
    )
    return result[0, 0]


def pair_count(tap_rows, share_rows, pair_rows, parts):
    most = 1
    for index in range(parts):
        first = index * share_rows
        last = first + share_rows - 1
        most = max(most, last // pair_rows - first // pair_rows + 1)
    return most


def block_weight_grad(hidden_all, cot_all, frame_index, share_rows, channels):
    frame_total, row_total, col_total, slots = cot_all.shape
    pair_rows = 3 * channels
    tap_rows = 27 * channels
    edged = jnp.pad(cot_all, ((0, 2), (1, 1), (1, 1), (0, 0)))
    shifted = jnp.stack(
        [edged[:, :, 2 - col_tap : 2 - col_tap + col_total] for col_tap in range(3)], axis=3
    )
    first_row = frame_index * share_rows
    first_pair = first_row // pair_rows
    count = pair_count(tap_rows, share_rows, pair_rows, tap_rows // share_rows)
    pieces = []
    for step in range(count):
        pair = jnp.minimum(first_pair + step, 8)
        depth_tap = pair // 3
        row_tap = pair % 3
        window = lax.dynamic_slice(
            shifted,
            (2 - depth_tap, 2 - row_tap, 0, 0, 0),
            (frame_total, row_total, col_total, 3, slots),
        )
        product = lax.dot_general(
            window, hidden_all, (((0, 1, 2), (0, 1, 2)), ((), ())),
            preferred_element_type=jnp.float32,
        )
        pieces.append(product.transpose(0, 2, 1).reshape(pair_rows, slots))
    stacked = jnp.concatenate(pieces, axis=0)
    return lax.dynamic_slice_in_dim(stacked, first_row - first_pair * pair_rows, share_rows, 0)


def gather_rows(own, height_count):
    frame_total, row_count, col_count, channels = own.shape
    height_index = lax.axis_index("height")
    core = height_index % 2
    chip = height_index // 2
    chips = height_count // 2
    first = core == 0
    sibling = [(i, i ^ 1) for i in range(height_count)]
    mine = [own] + [
        lax.ppermute(
            own, "height", [(i, (i + 2 * step) % height_count) for i in range(height_count)]
        )
        for step in range(1, chips)
    ]
    stacked = jnp.concatenate(mine, axis=1)
    twins = lax.ppermute(stacked, "height", sibling)
    block = 2 * row_count
    relative = []
    for step in reversed(range(chips)):
        ours = stacked[:, step * row_count : (step + 1) * row_count]
        theirs = twins[:, step * row_count : (step + 1) * row_count]
        relative.append(
            jnp.where(
                first,
                jnp.concatenate([ours, theirs], axis=1),
                jnp.concatenate([theirs, ours], axis=1),
            )
        )
    relative = jnp.concatenate(relative, axis=1)
    return jnp.concatenate(
        [
            lax.dynamic_slice_in_dim(relative, ((place - chip - 1) % chips) * block, block, 1)
            for place in range(chips)
        ],
        axis=1,
    )


def gather_frames(block, lead, carried):
    count = lax.axis_size("tm")
    position = lax.axis_index("tm")
    up = [(i, i + 1) for i in range(count - 1)]
    down = [(i + 1, i) for i in range(count - 1)]
    earlier, later = [], []
    rising, falling = block, block
    for step in range(1, count):
        rising = lax.ppermute(rising, "tm", up)
        if not carried(step) and falling.shape[-1] == block.shape[-1]:
            falling = falling[..., lead:]
        falling = lax.ppermute(falling, "tm", down)
        earlier.append(rising)
        if falling.shape[-1] == block.shape[-1]:
            later.append(falling)
        else:
            later.append(
                jnp.concatenate(
                    [jnp.zeros(falling.shape[:-1] + (lead,), falling.dtype), falling], axis=-1
                )
            )
    relative = jnp.concatenate(earlier[::-1] + [block] + later, axis=0)
    return lax.dynamic_slice_in_dim(relative, count - 1 - position, count * block.shape[0], 0)


def falling_hidden(total_frames, frame_devices, share_rows, channels):
    plane_rows = 9 * channels

    def deepest(device):
        return ((device + 1) * share_rows - 1) // plane_rows

    def carried(step):
        return any(
            frame <= total_frames - 3 + deepest(frame - step)
            for frame in range(step, frame_devices)
        )

    return carried


def local(latents, gain, bias, weight, cotangent):
    frame_count, row_count, col_count, channels = latents.shape
    latent_wide = latents.astype(jnp.float32)
    root_mean = jnp.sqrt(jnp.mean(latent_wide * latent_wide, axis=-1, keepdims=True) + 1e-06)
    normed = latent_wide / root_mean * gain
    hidden = jax.nn.silu(normed).astype(jnp.bfloat16)
    height_count = lax.axis_size("height")
    frame_devices = lax.axis_size("tm")
    frame_index = lax.axis_index("tm")
    row_index = lax.axis_index("height")
    total_rows = row_count * height_count
    total_frames = frame_count * frame_devices
    tap_rows = 27 * channels
    share_rows = tap_rows // frame_devices
    padded_cols = -(-(col_count + 2) // 8) * 8
    right_pad = padded_cols - col_count - 1
    inverse_root = 1.0 / math.sqrt(total_frames * total_rows * col_count)
    weight_cube = weight.reshape(3, 3, 3, channels, channels)

    both_frames = gather_frames(
        jnp.concatenate([hidden, cotangent], axis=-1),
        channels,
        falling_hidden(total_frames, frame_devices, share_rows, channels),
    )
    hidden_all = gather_rows(both_frames[..., :channels], height_count)

    cot_frames = both_frames[..., channels:]
    cot_all = lax.all_to_all(cot_frames, "height", split_axis=3, concat_axis=1, tiled=True)

    window = lax.dynamic_slice(
        jnp.pad(hidden_all, ((2, 0), (1, 1), (1, 1), (0, 0))),
        (frame_index * frame_count, row_index * row_count, 0, 0),
        (frame_count + 2, row_count + 2, col_count + 2, channels),
    )
    conv_out = forward_conv(window, weight_cube, row_count, col_count).reshape(
        frame_count, row_count, col_count, channels
    )
    output = (latent_wide + conv_out + bias).astype(jnp.bfloat16)

    weight_grad = (
        block_weight_grad(hidden_all, cot_all, frame_index, share_rows, channels) * inverse_root
    )

    cot_future = lax.dynamic_slice_in_dim(
        jnp.pad(cot_frames, ((0, 2), (0, 0), (0, 0), (0, 0))), frame_index * frame_count, 3, 0
    )
    cotangent_edged = padded(cot_future, (("height", 1),), 1)
    future_block = jnp.pad(cotangent_edged, ((0, 0), (0, 0), (1, right_pad), (0, 0)))
    hidden_grad = backward_conv(future_block, weight_cube, row_count, col_count).reshape(frame_count, row_count, col_count, channels)
    sigmoid_pre = jax.nn.sigmoid(normed)
    normed_grad = hidden_grad * sigmoid_pre * (1.0 + normed * (1.0 - sigmoid_pre))
    scaled_grad = normed_grad * gain
    unit_latent = latent_wide / root_mean
    inner = jnp.mean(scaled_grad * unit_latent, axis=-1, keepdims=True)
    latent_grad = (
        cotangent.astype(jnp.float32) + (scaled_grad - unit_latent * inner) / root_mean
    ).astype(jnp.bfloat16)
    return (output, latent_grad, weight_grad)


def solution(mesh):
    placed = (
        P(("grp", "tm"), "height", None, None),
        P(),
        P(),
        P(),
        P(("grp", "tm"), "height", None, None),
    )
    return jax.shard_map(
        local,
        mesh=mesh,
        in_specs=placed,
        out_specs=(
            P(("grp", "tm"), "height", None, None),
            P(("grp", "tm"), "height", None, None),
            P(("grp", "tm"), "height"),
        ),
        check_vma=False,
    )
```

```python
import math

import jax
import jax.numpy as jnp
from jax import lax
from jax.sharding import PartitionSpec as P


def shifted_2(value, axis, by):
    devices = lax.axis_size(axis)
    pairs = [(i, i + by) for i in range(devices) if 0 <= i + by < devices]
    return lax.ppermute(value, axis, pairs)


def padded(cells, sides, width):
    for axis, dim in sides:
        count = lax.axis_size(axis)
        ends = count - 1
        head = lax.slice_in_dim(cells, 0, width, axis=dim)
        tail = lax.slice_in_dim(cells, cells.shape[dim] - width, cells.shape[dim], axis=dim)
        cells = jnp.concatenate(
            [
                lax.ppermute(tail, axis, [(i, (i + 1) % count) for i in range(ends)]),
                cells,
                lax.ppermute(head, axis, [((i + 1) % count, i) for i in range(ends)]),
            ],
            axis=dim,
        )
    return cells


def forward_arrange(cube):
    depth, rows_t, cols_t, inputs, outputs = cube.shape
    return cube.transpose(0, 1, 3, 2, 4).reshape(9, inputs, 3 * outputs)


def backward_arrange(cube):
    depth, rows_t, cols_t, inputs, outputs = cube.shape
    return cube.transpose(0, 1, 4, 2, 3).reshape(9, outputs, 3 * inputs)


def forward_conv(window, cube, row_total, col_total):
    window = window[:, :, : col_total + 2]
    result = lax.conv_general_dilated(
        window[None],
        cube,
        (1, 1, 1),
        "VALID",
        dimension_numbers=("NDHWC", "DHWIO", "NDHWC"),
        preferred_element_type=jnp.float32,
    )
    return result[0, 0]


def backward_conv(window, cube, row_total, col_total):
    window = window[:, :, : col_total + 2]
    result = lax.conv_general_dilated(
        window[None],
        jnp.flip(cube, (0, 1, 2)),
        (1, 1, 1),
        "VALID",
        dimension_numbers=("NDHWC", "DHWOI", "NDHWC"),
        preferred_element_type=jnp.float32,
    )
    return result[0, 0]


def pair_count(tap_rows, share_rows, pair_rows, parts):
    most = 1
    for index in range(parts):
        first = index * share_rows
        last = first + share_rows - 1
        most = max(most, last // pair_rows - first // pair_rows + 1)
    return most


def block_weight_grad(hidden_all, cot_all, frame_index, share_rows, channels):
    frame_total, row_total, col_total, slots = cot_all.shape
    pair_rows = 3 * channels
    tap_rows = 27 * channels
    edged = jnp.pad(cot_all, ((0, 2), (1, 1), (1, 1), (0, 0)))
    shifted = jnp.stack(
        [edged[:, :, 2 - col_tap : 2 - col_tap + col_total] for col_tap in range(3)], axis=3
    )
    first_row = frame_index * share_rows
    first_pair = first_row // pair_rows
    count = pair_count(tap_rows, share_rows, pair_rows, tap_rows // share_rows)
    pieces = []
    for step in range(count):
        pair = jnp.minimum(first_pair + step, 8)
        depth_tap = pair // 3
        row_tap = pair % 3
        window = lax.dynamic_slice(
            shifted,
            (2 - depth_tap, 2 - row_tap, 0, 0, 0),
            (frame_total, row_total, col_total, 3, slots),
        )
        product = lax.dot_general(
            window, hidden_all, (((0, 1, 2), (0, 1, 2)), ((), ())),
            preferred_element_type=jnp.float32,
        )
        pieces.append(product.transpose(0, 2, 1).reshape(pair_rows, slots))
    stacked = jnp.concatenate(pieces, axis=0)
    return lax.dynamic_slice_in_dim(stacked, first_row - first_pair * pair_rows, share_rows, 0)


def gather_rows(own, height_count):
    frame_total, row_count, col_count, channels = own.shape
    height_index = lax.axis_index("height")
    core = height_index % 2
    chip = height_index // 2
    chips = height_count // 2
    first = core == 0
    sibling = [(i, i ^ 1) for i in range(height_count)]
    mine = [own] + [
        lax.ppermute(
            own, "height", [(i, (i + 2 * step) % height_count) for i in range(height_count)]
        )
        for step in range(1, chips)
    ]
    stacked = jnp.concatenate(mine, axis=1)
    twins = lax.ppermute(stacked, "height", sibling)
    block = 2 * row_count
    relative = []
    for step in reversed(range(chips)):
        ours = stacked[:, step * row_count : (step + 1) * row_count]
        theirs = twins[:, step * row_count : (step + 1) * row_count]
        relative.append(
            jnp.where(
                first,
                jnp.concatenate([ours, theirs], axis=1),
                jnp.concatenate([theirs, ours], axis=1),
            )
        )
    relative = jnp.concatenate(relative, axis=1)
    return jnp.concatenate(
        [
            lax.dynamic_slice_in_dim(relative, ((place - chip - 1) % chips) * block, block, 1)
            for place in range(chips)
        ],
        axis=1,
    )


def gather_frames(block):
    count = lax.axis_size("tm")
    position = lax.axis_index("tm")
    up = [(i, i + 1) for i in range(count - 1)]
    down = [(i + 1, i) for i in range(count - 1)]
    earlier, later = [], []
    rising, falling = block, block
    for step in range(1, count):
        rising = lax.ppermute(rising, "tm", up)
        falling = lax.ppermute(falling, "tm", down)
        earlier.append(rising)
        later.append(falling)
    relative = jnp.concatenate(earlier[::-1] + [block] + later, axis=0)
    return lax.dynamic_slice_in_dim(relative, count - 1 - position, count * block.shape[0], 0)


def local(latents, gain, bias, weight, cotangent):
    frame_count, row_count, col_count, channels = latents.shape
    latent_wide = latents.astype(jnp.float32)
    root_mean = jnp.sqrt(jnp.mean(latent_wide * latent_wide, axis=-1, keepdims=True) + 1e-06)
    normed = latent_wide / root_mean * gain
    hidden = jax.nn.silu(normed).astype(jnp.bfloat16)
    height_count = lax.axis_size("height")
    frame_devices = lax.axis_size("tm")
    frame_index = lax.axis_index("tm")
    row_index = lax.axis_index("height")
    total_rows = row_count * height_count
    total_frames = frame_count * frame_devices
    tap_rows = 27 * channels
    share_rows = tap_rows // frame_devices
    padded_cols = -(-(col_count + 2) // 8) * 8
    right_pad = padded_cols - col_count - 1
    inverse_root = 1.0 / math.sqrt(total_frames * total_rows * col_count)
    weight_cube = weight.reshape(3, 3, 3, channels, channels)

    both_frames = gather_frames(jnp.concatenate([hidden, cotangent], axis=-1))
    hidden_all = gather_rows(both_frames[..., :channels], height_count)

    cot_frames = both_frames[..., channels:]
    share_width = channels // height_count
    by_share = cot_frames.reshape(
        total_frames, row_count, col_count, height_count, share_width
    ).transpose(3, 0, 1, 2, 4)
    cot_all = (
        lax.all_to_all(by_share, "height", split_axis=0, concat_axis=0, tiled=True)
        .transpose(1, 0, 2, 3, 4)
        .reshape(total_frames, total_rows, col_count, share_width)
    )

    window = lax.dynamic_slice(
        jnp.pad(hidden_all, ((2, 0), (1, 1), (1, 1), (0, 0))),
        (frame_index * frame_count, row_index * row_count, 0, 0),
        (frame_count + 2, row_count + 2, col_count + 2, channels),
    )
    conv_out = forward_conv(window, weight_cube, row_count, col_count).reshape(
        frame_count, row_count, col_count, channels
    )
    output = (latent_wide + conv_out + bias).astype(jnp.bfloat16)

    weight_grad = (
        block_weight_grad(hidden_all, cot_all, frame_index, share_rows, channels) * inverse_root
    )

    cot_future = lax.dynamic_slice_in_dim(
        jnp.pad(cot_frames, ((0, 2), (0, 0), (0, 0), (0, 0))), frame_index * frame_count, 3, 0
    )
    cotangent_edged = padded(cot_future, (("height", 1),), 1)
    future_block = jnp.pad(cotangent_edged, ((0, 0), (0, 0), (1, right_pad), (0, 0)))
    hidden_grad = backward_conv(future_block, weight_cube, row_count, col_count).reshape(frame_count, row_count, col_count, channels)
    sigmoid_pre = jax.nn.sigmoid(normed)
    normed_grad = hidden_grad * sigmoid_pre * (1.0 + normed * (1.0 - sigmoid_pre))
    scaled_grad = normed_grad * gain
    unit_latent = latent_wide / root_mean
    inner = jnp.mean(scaled_grad * unit_latent, axis=-1, keepdims=True)
    latent_grad = (
        cotangent.astype(jnp.float32) + (scaled_grad - unit_latent * inner) / root_mean
    ).astype(jnp.bfloat16)
    return (output, latent_grad, weight_grad)


def solution(mesh):
    placed = (
        P(("grp", "tm"), "height", None, None),
        P(),
        P(),
        P(),
        P(("grp", "tm"), "height", None, None),
    )
    return jax.shard_map(
        local,
        mesh=mesh,
        in_specs=placed,
        out_specs=(
            P(("grp", "tm"), "height", None, None),
            P(("grp", "tm"), "height", None, None),
            P(("grp", "tm"), "height"),
        ),
        check_vma=False,
    )
```

```python
import math

import jax
import jax.numpy as jnp
from jax import lax
from jax.sharding import PartitionSpec as P


def shifted_2(value, axis, by):
    devices = lax.axis_size(axis)
    pairs = [(i, i + by) for i in range(devices) if 0 <= i + by < devices]
    return lax.ppermute(value, axis, pairs)


def padded(cells, sides, width):
    for axis, dim in sides:
        count = lax.axis_size(axis)
        ends = count - 1
        head = lax.slice_in_dim(cells, 0, width, axis=dim)
        tail = lax.slice_in_dim(cells, cells.shape[dim] - width, cells.shape[dim], axis=dim)
        cells = jnp.concatenate(
            [
                lax.ppermute(tail, axis, [(i, (i + 1) % count) for i in range(ends)]),
                cells,
                lax.ppermute(head, axis, [((i + 1) % count, i) for i in range(ends)]),
            ],
            axis=dim,
        )
    return cells


def forward_arrange(cube):
    depth, rows_t, cols_t, inputs, outputs = cube.shape
    return cube.transpose(0, 1, 3, 2, 4).reshape(9, inputs, 3 * outputs)


def backward_arrange(cube):
    depth, rows_t, cols_t, inputs, outputs = cube.shape
    return cube.transpose(0, 1, 4, 2, 3).reshape(9, outputs, 3 * inputs)


def forward_conv(window, cube, row_total, col_total):
    window = window[:, :, : col_total + 2]
    result = lax.conv_general_dilated(
        window[None],
        cube,
        (1, 1, 1),
        "VALID",
        dimension_numbers=("NDHWC", "DHWIO", "NDHWC"),
        preferred_element_type=jnp.float32,
    )
    return result[0, 0]


def backward_conv(window, cube, row_total, col_total):
    window = window[:, :, : col_total + 2]
    result = lax.conv_general_dilated(
        window[None],
        jnp.flip(cube, (0, 1, 2)),
        (1, 1, 1),
        "VALID",
        dimension_numbers=("NDHWC", "DHWOI", "NDHWC"),
        preferred_element_type=jnp.float32,
    )
    return result[0, 0]


def pair_count(tap_rows, share_rows, pair_rows, parts):
    most = 1
    for index in range(parts):
        first = index * share_rows
        last = first + share_rows - 1
        most = max(most, last // pair_rows - first // pair_rows + 1)
    return most


def block_weight_grad(hidden_all, cot_all, frame_index, share_rows, channels):
    frame_total, row_total, col_total, slots = cot_all.shape
    pair_rows = 3 * channels
    tap_rows = 27 * channels
    edged = jnp.pad(cot_all, ((0, 2), (1, 1), (1, 1), (0, 0)))
    shifted = jnp.stack(
        [edged[:, :, 2 - col_tap : 2 - col_tap + col_total] for col_tap in range(3)], axis=3
    )
    first_row = frame_index * share_rows
    first_pair = first_row // pair_rows
    count = pair_count(tap_rows, share_rows, pair_rows, tap_rows // share_rows)
    pieces = []
    for step in range(count):
        pair = jnp.minimum(first_pair + step, 8)
        depth_tap = pair // 3
        row_tap = pair % 3
        window = lax.dynamic_slice(
            shifted,
            (2 - depth_tap, 2 - row_tap, 0, 0, 0),
            (frame_total, row_total, col_total, 3, slots),
        )
        product = lax.dot_general(
            window, hidden_all, (((0, 1, 2), (0, 1, 2)), ((), ())),
            preferred_element_type=jnp.float32,
        )
        pieces.append(product.transpose(0, 2, 1).reshape(pair_rows, slots))
    stacked = jnp.concatenate(pieces, axis=0)
    return lax.dynamic_slice_in_dim(stacked, first_row - first_pair * pair_rows, share_rows, 0)


def gather_rows(own, height_count):
    frame_total, row_count, col_count, channels = own.shape
    height_index = lax.axis_index("height")
    core = height_index % 2
    chip = height_index // 2
    chips = height_count // 2
    first = core == 0
    sibling = [(i, i ^ 1) for i in range(height_count)]
    mine = [own] + [
        lax.ppermute(
            own, "height", [(i, (i + 2 * step) % height_count) for i in range(height_count)]
        )
        for step in range(1, chips)
    ]
    stacked = jnp.concatenate(mine, axis=1)
    twins = lax.ppermute(stacked, "height", sibling)
    lower = jnp.where(first, stacked, twins)
    upper = jnp.where(first, twins, stacked)
    blocks = []
    for place in range(chips):
        step = (chip - place) % chips
        for half in (lower, upper):
            blocks.append(lax.dynamic_slice_in_dim(half, step * row_count, row_count, 1))
    return jnp.concatenate(blocks, axis=1)


def gather_frames(block):
    count = lax.axis_size("tm")
    position = lax.axis_index("tm")
    up = [(i, i + 1) for i in range(count - 1)]
    down = [(i + 1, i) for i in range(count - 1)]
    earlier, later = [], []
    rising, falling = block, block
    for step in range(1, count):
        rising = lax.ppermute(rising, "tm", up)
        falling = lax.ppermute(falling, "tm", down)
        earlier.append(rising)
        later.append(falling)
    relative = jnp.concatenate(earlier[::-1] + [block] + later, axis=0)
    return lax.dynamic_slice_in_dim(relative, count - 1 - position, count * block.shape[0], 0)


def local(latents, gain, bias, weight, cotangent):
    frame_count, row_count, col_count, channels = latents.shape
    latent_wide = latents.astype(jnp.float32)
    root_mean = jnp.sqrt(jnp.mean(latent_wide * latent_wide, axis=-1, keepdims=True) + 1e-06)
    normed = latent_wide / root_mean * gain
    hidden = jax.nn.silu(normed).astype(jnp.bfloat16)
    height_count = lax.axis_size("height")
    frame_devices = lax.axis_size("tm")
    frame_index = lax.axis_index("tm")
    row_index = lax.axis_index("height")
    total_rows = row_count * height_count
    total_frames = frame_count * frame_devices
    tap_rows = 27 * channels
    share_rows = tap_rows // frame_devices
    padded_cols = -(-(col_count + 2) // 8) * 8
    right_pad = padded_cols - col_count - 1
    inverse_root = 1.0 / math.sqrt(total_frames * total_rows * col_count)
    weight_cube = weight.reshape(3, 3, 3, channels, channels)

    both_frames = gather_frames(jnp.concatenate([hidden, cotangent], axis=-1))
    hidden_all = gather_rows(both_frames[..., :channels], height_count)

    cot_frames = both_frames[..., channels:]
    share_width = channels // height_count
    by_share = cot_frames.reshape(
        total_frames, row_count, col_count, height_count, share_width
    ).transpose(3, 0, 1, 2, 4)
    cot_all = (
        lax.all_to_all(by_share, "height", split_axis=0, concat_axis=0, tiled=True)
        .transpose(1, 0, 2, 3, 4)
        .reshape(total_frames, total_rows, col_count, share_width)
    )

    window = lax.dynamic_slice(
        jnp.pad(hidden_all, ((2, 0), (1, 1), (1, 1), (0, 0))),
        (frame_index * frame_count, row_index * row_count, 0, 0),
        (frame_count + 2, row_count + 2, col_count + 2, channels),
    )
    conv_out = forward_conv(window, weight_cube, row_count, col_count).reshape(
        frame_count, row_count, col_count, channels
    )
    output = (latent_wide + conv_out + bias).astype(jnp.bfloat16)

    weight_grad = (
        block_weight_grad(hidden_all, cot_all, frame_index, share_rows, channels) * inverse_root
    )

    cot_future = lax.dynamic_slice_in_dim(
        jnp.pad(cot_frames, ((0, 2), (0, 0), (0, 0), (0, 0))), frame_index * frame_count, 3, 0
    )
    cotangent_edged = padded(cot_future, (("height", 1),), 1)
    future_block = jnp.pad(cotangent_edged, ((0, 0), (0, 0), (1, right_pad), (0, 0)))
    hidden_grad = backward_conv(future_block, weight_cube, row_count, col_count).reshape(frame_count, row_count, col_count, channels)
    sigmoid_pre = jax.nn.sigmoid(normed)
    normed_grad = hidden_grad * sigmoid_pre * (1.0 + normed * (1.0 - sigmoid_pre))
    scaled_grad = normed_grad * gain
    unit_latent = latent_wide / root_mean
    inner = jnp.mean(scaled_grad * unit_latent, axis=-1, keepdims=True)
    latent_grad = (
        cotangent.astype(jnp.float32) + (scaled_grad - unit_latent * inner) / root_mean
    ).astype(jnp.bfloat16)
    return (output, latent_grad, weight_grad)


def solution(mesh):
    placed = (
        P(("grp", "tm"), "height", None, None),
        P(),
        P(),
        P(),
        P(("grp", "tm"), "height", None, None),
    )
    return jax.shard_map(
        local,
        mesh=mesh,
        in_specs=placed,
        out_specs=(
            P(("grp", "tm"), "height", None, None),
            P(("grp", "tm"), "height", None, None),
            P(("grp", "tm"), "height"),
        ),
        check_vma=False,
    )
```

```python
import math

import jax
import jax.numpy as jnp
from jax import lax
from jax.sharding import PartitionSpec as P


def shifted_2(value, axis, by):
    devices = lax.axis_size(axis)
    pairs = [(i, i + by) for i in range(devices) if 0 <= i + by < devices]
    return lax.ppermute(value, axis, pairs)


def padded(cells, sides, width):
    for axis, dim in sides:
        count = lax.axis_size(axis)
        ends = count - 1
        head = lax.slice_in_dim(cells, 0, width, axis=dim)
        tail = lax.slice_in_dim(cells, cells.shape[dim] - width, cells.shape[dim], axis=dim)
        cells = jnp.concatenate(
            [
                lax.ppermute(tail, axis, [(i, (i + 1) % count) for i in range(ends)]),
                cells,
                lax.ppermute(head, axis, [((i + 1) % count, i) for i in range(ends)]),
            ],
            axis=dim,
        )
    return cells


def forward_arrange(cube):
    depth, rows_t, cols_t, inputs, outputs = cube.shape
    return cube.transpose(0, 1, 3, 2, 4).reshape(9, inputs, 3 * outputs)


def backward_arrange(cube):
    depth, rows_t, cols_t, inputs, outputs = cube.shape
    return cube.transpose(0, 1, 4, 2, 3).reshape(9, outputs, 3 * inputs)


def forward_conv(window, cube, row_total, col_total):
    window = window[:, :, : col_total + 2]
    result = lax.conv_general_dilated(
        window[None],
        cube,
        (1, 1, 1),
        "VALID",
        dimension_numbers=("NDHWC", "DHWIO", "NDHWC"),
        preferred_element_type=jnp.float32,
    )
    return result[0, 0]


def backward_conv(window, cube, row_total, col_total):
    window = window[:, :, : col_total + 2]
    result = lax.conv_general_dilated(
        window[None],
        jnp.flip(cube, (0, 1, 2)),
        (1, 1, 1),
        "VALID",
        dimension_numbers=("NDHWC", "DHWOI", "NDHWC"),
        preferred_element_type=jnp.float32,
    )
    return result[0, 0]


def pair_count(tap_rows, share_rows, pair_rows, parts):
    most = 1
    for index in range(parts):
        first = index * share_rows
        last = first + share_rows - 1
        most = max(most, last // pair_rows - first // pair_rows + 1)
    return most


def block_weight_grad(hidden_all, cot_all, frame_index, share_rows, channels):
    frame_total, row_total, col_total, slots = cot_all.shape
    pair_rows = 3 * channels
    tap_rows = 27 * channels
    edged = jnp.pad(cot_all, ((0, 2), (1, 1), (1, 1), (0, 0)))
    shifted = jnp.stack(
        [edged[:, :, 2 - col_tap : 2 - col_tap + col_total] for col_tap in range(3)], axis=3
    )
    first_row = frame_index * share_rows
    first_pair = first_row // pair_rows
    count = pair_count(tap_rows, share_rows, pair_rows, tap_rows // share_rows)
    pieces = []
    for step in range(count):
        pair = jnp.minimum(first_pair + step, 8)
        depth_tap = pair // 3
        row_tap = pair % 3
        window = lax.dynamic_slice(
            shifted,
            (2 - depth_tap, 2 - row_tap, 0, 0, 0),
            (frame_total, row_total, col_total, 3, slots),
        )
        product = lax.dot_general(
            window, hidden_all, (((0, 1, 2), (0, 1, 2)), ((), ())),
            preferred_element_type=jnp.float32,
        )
        pieces.append(product.transpose(0, 2, 1).reshape(pair_rows, slots))
    stacked = jnp.concatenate(pieces, axis=0)
    return lax.dynamic_slice_in_dim(stacked, first_row - first_pair * pair_rows, share_rows, 0)


def gather_rows(own, height_count):
    frame_total, row_count, col_count, channels = own.shape
    height_index = lax.axis_index("height")
    core = height_index % 2
    chip = height_index // 2
    chips = height_count // 2
    first = core == 0
    sibling = [(i, i ^ 1) for i in range(height_count)]
    mine = [own] + [
        lax.ppermute(
            own, "height", [(i, (i + 2 * step) % height_count) for i in range(height_count)]
        )
        for step in range(1, chips)
    ]
    stacked = jnp.concatenate(mine, axis=1)
    twins = lax.ppermute(stacked, "height", sibling)
    lower = jnp.where(first, stacked, twins)
    upper = jnp.where(first, twins, stacked)
    blocks = []
    for place in range(chips):
        step = (chip - place) % chips
        for half in (lower, upper):
            blocks.append(lax.dynamic_slice_in_dim(half, step * row_count, row_count, 1))
    return jnp.concatenate(blocks, axis=1)


def gather_frames(block):
    count = lax.axis_size("tm")
    position = lax.axis_index("tm")
    up = [(i, i + 1) for i in range(count - 1)]
    down = [(i + 1, i) for i in range(count - 1)]
    earlier, later = [], []
    rising, falling = block, block
    for step in range(1, count):
        rising = lax.ppermute(rising, "tm", up)
        falling = lax.ppermute(falling, "tm", down)
        earlier.append(rising)
        later.append(falling)
    relative = jnp.concatenate(earlier[::-1] + [block] + later, axis=0)
    return lax.dynamic_slice_in_dim(relative, count - 1 - position, count * block.shape[0], 0)


def local(latents, gain, bias, weight, cotangent):
    frame_count, row_count, col_count, channels = latents.shape
    latent_wide = latents.astype(jnp.float32)
    root_mean = jnp.sqrt(jnp.mean(latent_wide * latent_wide, axis=-1, keepdims=True) + 1e-06)
    normed = latent_wide / root_mean * gain
    hidden = jax.nn.silu(normed).astype(jnp.bfloat16)
    height_count = lax.axis_size("height")
    frame_devices = lax.axis_size("tm")
    frame_index = lax.axis_index("tm")
    row_index = lax.axis_index("height")
    total_rows = row_count * height_count
    total_frames = frame_count * frame_devices
    tap_rows = 27 * channels
    share_rows = tap_rows // frame_devices
    padded_cols = -(-(col_count + 2) // 8) * 8
    right_pad = padded_cols - col_count - 1
    inverse_root = 1.0 / math.sqrt(total_frames * total_rows * col_count)
    weight_cube = weight.reshape(3, 3, 3, channels, channels)

    both_frames = gather_frames(jnp.concatenate([hidden, cotangent], axis=-1))
    cot_frames = both_frames[..., channels:]
    cot_future = lax.dynamic_slice_in_dim(
        jnp.pad(cot_frames, ((0, 2), (0, 0), (0, 0), (0, 0))), frame_index * frame_count, 3, 0
    )
    cotangent_edged = padded(cot_future, (("height", 1),), 1)
    hidden_rows, cotangent_edged = lax.optimization_barrier(
        (both_frames[..., :channels], cotangent_edged)
    )
    hidden_all = gather_rows(hidden_rows, height_count)

    share_width = channels // height_count
    by_share = cot_frames.reshape(
        total_frames, row_count, col_count, height_count, share_width
    ).transpose(3, 0, 1, 2, 4)
    cot_all = (
        lax.all_to_all(by_share, "height", split_axis=0, concat_axis=0, tiled=True)
        .transpose(1, 0, 2, 3, 4)
        .reshape(total_frames, total_rows, col_count, share_width)
    )

    window = lax.dynamic_slice(
        jnp.pad(hidden_all, ((2, 0), (1, 1), (1, 1), (0, 0))),
        (frame_index * frame_count, row_index * row_count, 0, 0),
        (frame_count + 2, row_count + 2, col_count + 2, channels),
    )
    conv_out = forward_conv(window, weight_cube, row_count, col_count).reshape(
        frame_count, row_count, col_count, channels
    )
    output = (latent_wide + conv_out + bias).astype(jnp.bfloat16)

    weight_grad = (
        block_weight_grad(hidden_all, cot_all, frame_index, share_rows, channels) * inverse_root
    )

    future_block = jnp.pad(cotangent_edged, ((0, 0), (0, 0), (1, right_pad), (0, 0)))
    hidden_grad = backward_conv(future_block, weight_cube, row_count, col_count).reshape(frame_count, row_count, col_count, channels)
    sigmoid_pre = jax.nn.sigmoid(normed)
    normed_grad = hidden_grad * sigmoid_pre * (1.0 + normed * (1.0 - sigmoid_pre))
    scaled_grad = normed_grad * gain
    unit_latent = latent_wide / root_mean
    inner = jnp.mean(scaled_grad * unit_latent, axis=-1, keepdims=True)
    latent_grad = (
        cotangent.astype(jnp.float32) + (scaled_grad - unit_latent * inner) / root_mean
    ).astype(jnp.bfloat16)
    return (output, latent_grad, weight_grad)


def solution(mesh):
    placed = (
        P(("grp", "tm"), "height", None, None),
        P(),
        P(),
        P(),
        P(("grp", "tm"), "height", None, None),
    )
    return jax.shard_map(
        local,
        mesh=mesh,
        in_specs=placed,
        out_specs=(
            P(("grp", "tm"), "height", None, None),
            P(("grp", "tm"), "height", None, None),
            P(("grp", "tm"), "height"),
        ),
        check_vma=False,
    )
```
